128 devices in a mesh: replica: 8 (over z, y_lo), fsdp: 16 (over y_hi, x, core).
Axes of the slice: x: 4, y: 4 (y_hi: 2, y_lo: 2; y = y_hi * 2 + y_lo), z: 4, core: 2. Of those that a mesh axis runs over, the one named last changes fastest.
Arguments:
- tokens: bfloat16 [8, 2048, 4096], P('replica', 'fsdp'), may hold values from -6 to 6
- queries: bfloat16 [8, 2048, 4096], P('replica', 'fsdp'), may hold values from -64 to 64
- keys: bfloat16 [8, 2048, 512], P('replica', 'fsdp'), may hold values from -4 to 4
- value_weight: bfloat16 [4096, 512], P('fsdp'), may hold values from -4 to 4
- ctx_grad: bfloat16 [8, 2048, 4096], P('replica', 'fsdp'), may hold values from -6 to 6
- frag_global: float32 [4096, 2048], P('fsdp', 'replica'), may hold values from -4 to 4
- frag_momentum: float32 [4096, 2048], P('fsdp', 'replica'), may hold values from -1.8 to 1.8
- frag_local: bfloat16 [8, 4096, 2048], P('replica', 'fsdp'), may hold values from -6 to 6
Outputs:
- context: bfloat16 [8, 2048, 4096], P('replica', 'fsdp')
- query_grad: bfloat16 [8, 2048, 4096], P('replica', 'fsdp')
- key_grad: bfloat16 [8, 2048, 512], P('replica', 'fsdp')
- weight_grad: float32 [8, 4096, 512], P('replica', 'fsdp')
- token_grad: bfloat16 [8, 2048, 4096], P('replica', 'fsdp')
- new_global: float32 [4096, 2048], P('fsdp', 'replica')
- new_momentum: float32 [4096, 2048], P('fsdp', 'replica')
- refreshed_local: bfloat16 [4096, 2048], P('fsdp')
The draws below stay inside these ranges and needn't reach their ends.
All inputs are finite; a program needn't handle non-finite values.
Results may differ from the reference program's by a relative error of at most 0.02.
Values may be sent and summed in bfloat16 or wider, within the bound.
No kernel may reach another device: no remote copies, remote signals or barrier semaphores. Data moves between devices by JAX's collectives and lax.ppermute only.
A program may use at most 192 MiB of HBM per device.

```python
import jax
import jax.numpy as jnp
from jax import lax

D = 4096
HEADS = 32
KVH = 4
HD = 128
FRAGW = 2048
TOK_DEV = 128
LENGTH = 2048
REPLICAS = 8


def attention_pair(key):
    query_key = jax.random.fold_in(key, 101)
    keys_key = jax.random.fold_in(key, 102)
    query_width = HEADS * HD
    key_width = KVH * HD
    query_out = jnp.clip(jax.random.normal(query_key, (LENGTH, query_width), jnp.float32), -4.0, 4.0)
    keys_out = jnp.clip(jax.random.normal(keys_key, (LENGTH, key_width), jnp.float32), -4.0, 4.0)
    return (query_out, keys_out)


def attention_all(key):

    def one_replica(index):
        return attention_pair(jax.random.fold_in(key, index))
    return jax.vmap(one_replica)(jnp.arange(REPLICAS))


def draw_queries(key, part):
    return attention_all(key)[0].astype(jnp.bfloat16)


def draw_keys(key, part):
    return attention_all(key)[1].astype(jnp.bfloat16)


def fragment_pair(key):
    base_key = jax.random.fold_in(key, 201)
    drift_key = jax.random.fold_in(key, 202)
    own_drift = jax.random.normal(drift_key, (REPLICAS, D, FRAGW), jnp.float32)
    base = jnp.clip(jax.random.normal(base_key, (D, FRAGW), jnp.float32), -4.0, 4.0)
    drift = 0.25 * own_drift
    drift = jnp.clip(drift, -1.5, 1.5)
    return (base, base[None] + drift)


def draw_frag_global(key, part):
    return fragment_pair(key)[0]


def draw_frag_local(key, part):
    return fragment_pair(key)[1].astype(jnp.bfloat16)


def strengthened(values, rng, source, target, parts, factor):
    def block_of(axis_at):
        return (jnp.arange(values.shape[axis_at]) // (values.shape[axis_at] // parts)).reshape((-1,) + (1,) * (values.ndim - 1 - axis_at))

    near = jax.random.permutation(rng, parts)[block_of(target)]
    second = (block_of(target) + parts // 2) % parts
    return jnp.where((block_of(source) == near) | (block_of(source) == second), factor * values, values)


def levels(key, dims, cuts, low, top_value):
    def one(position, shards_of):
        heights = jax.random.uniform(jax.random.fold_in(jax.random.fold_in(key, 6), position), (shards_of,), jnp.float32, low / len(cuts), top_value / len(cuts))
        return jnp.repeat(jnp.exp(heights), dims[position] // shards_of).reshape((-1,) + (1,) * (len(dims) - position - 1))

    level = one(*cuts[0])
    for cut in cuts[1:]:
        level = level * one(*cut)
    return level


def noise(stream_key, shape, spread, limit, cuts=(), kind=jnp.bfloat16):
    entries = spread * jax.random.normal(stream_key, shape, jnp.float32)
    if cuts:
        entries = entries * levels(stream_key, shape, cuts, -0.22, 0.18)
    return jnp.clip(entries, -limit, limit).astype(kind)


def noise_with(key, dims, spread, most, pieces, heavy, held_as=jnp.bfloat16):
    values = spread * jax.random.normal(key, dims, jnp.float32)
    if pieces:
        values = values * levels(key, dims, pieces, -0.22, 0.18)
    return jnp.clip(strengthened(values, jax.random.fold_in(key, 3), *heavy), -most, most).astype(held_as)


def setup_inputs(seed: int = 0) -> dict:
    key_list = jax.random.split(jax.random.key(seed), 9)
    return {
        "tokens": noise_with(key_list[0], (REPLICAS, LENGTH, D), 1.0, 6.0, ((0, 8), (1, 16)), (1, 2, 16, 2.0)),
        "queries": draw_queries(jax.random.fold_in(key_list[8], 71), 0),
        "keys": draw_keys(jax.random.fold_in(key_list[8], 71), 0),
        "value_weight": noise(key_list[3], (D, KVH * HD), 1.0, 4.0, ((0, 16),)),
        "ctx_grad": noise(key_list[4], (REPLICAS, LENGTH, HEADS * HD), 1.0, 6.0, ((0, 8), (1, 16))),
        "frag_global": draw_frag_global(jax.random.fold_in(key_list[8], 71), 0),
        "frag_momentum": noise(key_list[6], (D, FRAGW), 0.3, 1.8, ((0, 16), (1, 8)), jnp.float32),
        "frag_local": draw_frag_local(jax.random.fold_in(key_list[8], 71), 0),
    }


outer_momentum = 0.9
outer_rate = 0.7
masked_score = -1.0e30


def reference(tokens, queries, keys, value_weight, ctx_grad, frag_global, frag_momentum, frag_local):
    proj_scale = D ** -0.5
    score_scale = HD ** -0.5
    group = HEADS // KVH
    blocks = LENGTH // TOK_DEV
    positions = jnp.arange(LENGTH)
    causal = positions[None, :] <= positions[:, None]

    def one_group(operands):
        query_part, key_part, value_part, grad_part = operands
        query_f = query_part.astype(jnp.float32)
        key_f = key_part.astype(jnp.float32)
        value_f = value_part.astype(jnp.float32)
        grad_f = grad_part.astype(jnp.float32)
        scores = jnp.einsum('thd,kd->htk', query_f, key_f) * score_scale
        scores = jnp.where(causal[None], scores, masked_score)
        top = jnp.max(scores, axis=-1, keepdims=True)
        summed = jnp.sum(jnp.exp(scores - top), axis=-1, keepdims=True)
        log_total = top + jnp.log(summed)
        probs = jnp.exp(scores - log_total)
        probs_low = lax.optimization_barrier(probs.astype(jnp.bfloat16)).astype(jnp.float32)
        context_part = jnp.einsum('htk,kd->thd', probs_low, value_f).astype(jnp.bfloat16)
        dprobs = jnp.einsum('thd,kd->htk', grad_f, value_f)
        rowdot = jnp.sum(grad_f * context_part.astype(jnp.float32), axis=-1).transpose(1, 0)[:, :, None]
        dscores = lax.optimization_barrier((probs * (dprobs - rowdot) * score_scale).astype(jnp.bfloat16)).astype(jnp.float32)
        query_part_grad = jnp.einsum('htk,kd->thd', dscores, key_f).astype(jnp.bfloat16)
        dscores_blocks = dscores.reshape(group, blocks, TOK_DEV, LENGTH)
        probs_blocks = probs_low.reshape(group, blocks, TOK_DEV, LENGTH)
        key_partials = jnp.einsum('hntk,nthd->nkd', dscores_blocks, query_f.reshape(blocks, TOK_DEV, group, HD))
        value_partials = jnp.einsum('hntk,nthd->nkd', probs_blocks, grad_f.reshape(blocks, TOK_DEV, group, HD))
        key_sum = jnp.sum(key_partials.astype(jnp.bfloat16).astype(jnp.float32), axis=0)
        value_sum = jnp.sum(value_partials.astype(jnp.bfloat16).astype(jnp.float32), axis=0)
        return context_part, query_part_grad, key_sum.astype(jnp.bfloat16), value_sum.astype(jnp.bfloat16)

    def one_sequence(operands):
        seq_tokens, seq_queries, seq_keys, seq_grad = operands
        values = (jnp.dot(seq_tokens, value_weight, preferred_element_type=jnp.float32) * proj_scale).astype(jnp.bfloat16)
        query_groups = seq_queries.reshape(LENGTH, KVH, group, HD).transpose(1, 0, 2, 3)
        key_groups = seq_keys.reshape(LENGTH, KVH, HD).transpose(1, 0, 2)
        value_groups = values.reshape(LENGTH, KVH, HD).transpose(1, 0, 2)
        grad_groups = seq_grad.reshape(LENGTH, KVH, group, HD).transpose(1, 0, 2, 3)
        context_all, query_all, key_all, value_all = lax.map(one_group, (query_groups, key_groups, value_groups, grad_groups))
        context = context_all.transpose(1, 0, 2, 3).reshape(LENGTH, HEADS * HD)
        query_grad = query_all.transpose(1, 0, 2, 3).reshape(LENGTH, HEADS * HD)
        key_grad = key_all.transpose(1, 0, 2).reshape(LENGTH, KVH * HD)
        value_grad = value_all.transpose(1, 0, 2).reshape(LENGTH, KVH * HD)
        token_blocks = seq_tokens.reshape(blocks, TOK_DEV, D).astype(jnp.float32)
        value_blocks = value_grad.reshape(blocks, TOK_DEV, KVH * HD).astype(jnp.float32)
        weight_partials = jnp.einsum('ntd,ntc->ndc', token_blocks, value_blocks) * proj_scale
        weight_grad = jnp.sum(weight_partials.astype(jnp.bfloat16).astype(jnp.float32), axis=0)
        token_grad = (jnp.dot(value_grad, value_weight.T, preferred_element_type=jnp.float32) * proj_scale).astype(jnp.bfloat16)
        return context, query_grad, key_grad, weight_grad, token_grad

    context, query_grad, key_grad, weight_grad, token_grad = lax.map(one_sequence, (tokens, queries, keys, ctx_grad))
    mean_local = jnp.sum(frag_local.astype(jnp.float32), axis=0) / REPLICAS
    delta = frag_global - mean_local
    new_momentum = outer_momentum * frag_momentum + delta
    new_global = frag_global - outer_rate * (delta + outer_momentum * new_momentum)
    refreshed_local = new_global.astype(jnp.bfloat16)
    return (context, query_grad, key_grad, weight_grad, token_grad, new_global, new_momentum, refreshed_local)
```

```python
import jax
import jax.numpy as jnp
from jax import lax
from jax.sharding import PartitionSpec as P

HD = 128


outer_momentum = 0.9
outer_rate = 0.7
masked_score = -1e30


def on_device(
    tokens, queries, keys, value_weight, ctx_grad, frag_global, frag_momentum, frag_local
):
    tokens = tokens[0]
    queries = queries[0]
    keys = keys[0]
    ctx_grad = ctx_grad[0]
    tok_rows = tokens.shape[0]
    model_width = tokens.shape[1]
    proj_scale = model_width ** (-0.5)
    score_scale = HD ** (-0.5)
    kv_heads = keys.shape[1] // HD
    group = queries.shape[1] // (kv_heads * HD)
    key_rows = keys.shape[0]
    weight_rows = value_weight.shape[0]
    fsdp_size = lax.axis_size("fsdp")
    gathered = lax.all_gather(
        jnp.concatenate([keys, value_weight], axis=0), "fsdp", axis=0, tiled=False
    )
    keys_all = gathered[:, :key_rows].reshape(fsdp_size * key_rows, keys.shape[1])
    weight_all = gathered[:, key_rows:].reshape(fsdp_size * weight_rows, value_weight.shape[1])
    value_sum = jnp.dot(tokens, weight_all, preferred_element_type=jnp.float32)
    values = (value_sum * proj_scale).astype(jnp.bfloat16)
    values_all = lax.all_gather(values, "fsdp", axis=0, tiled=True)
    length_all = keys_all.shape[0]
    query_pos = lax.axis_index("fsdp") * tok_rows + jnp.arange(tok_rows)
    causal = jnp.arange(length_all)[None, :] <= query_pos[:, None]
    query_heads = queries.reshape(tok_rows, kv_heads, group, HD)
    grad_heads = ctx_grad.reshape(tok_rows, kv_heads, group, HD)
    context_list = []
    query_list = []
    key_terms = []
    value_terms = []
    for group_index in range(kv_heads):
        query_part = query_heads[:, group_index]
        grad_part = grad_heads[:, group_index]
        key_part = keys_all[:, group_index * HD : (group_index + 1) * HD]
        value_part = values_all[:, group_index * HD : (group_index + 1) * HD]
        scores = (
            jnp.einsum("thd,kd->htk", query_part, key_part, preferred_element_type=jnp.float32)
            * score_scale
        )
        scores = jnp.where(causal[None], scores, masked_score)
        top = jnp.max(scores, axis=-1, keepdims=True)
        summed = jnp.sum(jnp.exp(scores - top), axis=-1, keepdims=True)
        log_total = top + jnp.log(summed)
        probs = jnp.exp(scores - log_total)
        probs_low = probs.astype(jnp.bfloat16)
        context_part = jnp.einsum(
            "htk,kd->thd", probs_low, value_part, preferred_element_type=jnp.float32
        ).astype(jnp.bfloat16)
        dprobs = jnp.einsum(
            "thd,kd->htk", grad_part, value_part, preferred_element_type=jnp.float32
        )
        rowdot = jnp.sum(
            grad_part.astype(jnp.float32) * context_part.astype(jnp.float32), axis=-1
        ).transpose(1, 0)[:, :, None]
        dscores = (probs * (dprobs - rowdot) * score_scale).astype(jnp.bfloat16)
        query_list.append(
            jnp.einsum("htk,kd->thd", dscores, key_part, preferred_element_type=jnp.float32).astype(
                jnp.bfloat16
            )
        )
        key_terms.append(
            jnp.einsum("htk,thd->kd", dscores, query_part, preferred_element_type=jnp.float32)
        )
        value_terms.append(
            jnp.einsum("htk,thd->kd", probs_low, grad_part, preferred_element_type=jnp.float32)
        )
        context_list.append(context_part)
    context = jnp.stack(context_list, axis=1).reshape(tok_rows, queries.shape[1])
    query_grad = jnp.stack(query_list, axis=1).reshape(tok_rows, queries.shape[1])
    key_term = jnp.concatenate(key_terms, axis=1)
    value_term = jnp.concatenate(value_terms, axis=1)
    kv_width = key_term.shape[1]
    kv_total = lax.psum_scatter(
        jnp.concatenate([key_term, value_term], axis=1).astype(jnp.bfloat16),
        "fsdp",
        scatter_dimension=0,
        tiled=True,
    ).astype(jnp.float32)
    key_sum = kv_total[:, :kv_width]
    value_total = kv_total[:, kv_width:]
    key_grad = key_sum.astype(jnp.bfloat16)
    value_grad = value_total.astype(jnp.bfloat16)
    product = lax.dot_general(
        tokens, value_grad, (((0,), (0,)), ((), ())), preferred_element_type=jnp.float32
    )
    weight_grad = lax.psum_scatter(
        (product * proj_scale).astype(jnp.bfloat16), "fsdp", scatter_dimension=0, tiled=True
    ).astype(jnp.float32)
    token_sum = lax.dot_general(
        value_grad,
        weight_all,
        (((1,), (1,)), ((), ())),
        preferred_element_type=jnp.float32,
    )
    token_grad = (token_sum * proj_scale).astype(jnp.bfloat16)
    replicas = lax.axis_size("replica")
    local_term = frag_local[0].astype(jnp.float32)
    own_sum = lax.psum_scatter(local_term, "replica", scatter_dimension=1, tiled=True)
    delta = frag_global - own_sum / replicas
    new_momentum = outer_momentum * frag_momentum + delta
    new_global = frag_global - outer_rate * (delta + outer_momentum * new_momentum)
    refreshed_local = lax.all_gather(new_global.astype(jnp.bfloat16), "replica", axis=1, tiled=True)
    return (
        context[None],
        query_grad[None],
        key_grad[None],
        weight_grad[None],
        token_grad[None],
        new_global,
        new_momentum,
        refreshed_local,
    )


def solution(mesh):
    return jax.shard_map(
        on_device,
        mesh=mesh,
        in_specs=(
            P("replica", "fsdp", None),
            P("replica", "fsdp", None),
            P("replica", "fsdp", None),
            P("fsdp", None),
            P("replica", "fsdp", None),
            P("fsdp", "replica"),
            P("fsdp", "replica"),
            P("replica", "fsdp", None),
        ),
        out_specs=(
            P("replica", "fsdp", None),
            P("replica", "fsdp", None),
            P("replica", "fsdp", None),
            P("replica", "fsdp", None),
            P("replica", "fsdp", None),
            P("fsdp", "replica"),
            P("fsdp", "replica"),
            P("fsdp", None),
        ),
        check_vma=False,
    )
```

```python
import jax
import jax.numpy as jnp
from jax import lax
from jax.sharding import PartitionSpec as P

HD = 128


outer_momentum = 0.9
outer_rate = 0.7
masked_score = -1e30


def on_device(
    tokens, queries, keys, value_weight, ctx_grad, frag_global, frag_momentum, frag_local
):
    tokens = tokens[0]
    queries = queries[0]
    keys = keys[0]
    ctx_grad = ctx_grad[0]
    tok_rows = tokens.shape[0]
    model_width = tokens.shape[1]
    proj_scale = model_width ** (-0.5)
    score_scale = HD ** (-0.5)
    kv_heads = keys.shape[1] // HD
    group = queries.shape[1] // (kv_heads * HD)
    key_rows = keys.shape[0]
    weight_rows = value_weight.shape[0]
    fsdp_size = lax.axis_size("fsdp")
    gathered = lax.all_gather(
        jnp.concatenate([keys, value_weight], axis=0), "fsdp", axis=0, tiled=False
    )
    keys_all = gathered[:, :key_rows].reshape(fsdp_size * key_rows, keys.shape[1])
    weight_all = gathered[:, key_rows:].reshape(fsdp_size * weight_rows, value_weight.shape[1])
    value_sum = jnp.dot(tokens, weight_all, preferred_element_type=jnp.float32)
    values = (value_sum * proj_scale).astype(jnp.bfloat16)
    values_all = lax.all_gather(values, "fsdp", axis=0, tiled=True)
    length_all = keys_all.shape[0]
    query_pos = lax.axis_index("fsdp") * tok_rows + jnp.arange(tok_rows)
    causal = jnp.arange(length_all)[None, :] <= query_pos[:, None]
    query_heads = queries.reshape(tok_rows, kv_heads, group, HD)
    grad_heads = ctx_grad.reshape(tok_rows, kv_heads, group, HD)
    context_list = []
    query_list = []
    key_terms = []
    value_terms = []
    for group_index in range(kv_heads):
        query_part = query_heads[:, group_index]
        grad_part = grad_heads[:, group_index]
        key_part = keys_all[:, group_index * HD : (group_index + 1) * HD]
        value_part = values_all[:, group_index * HD : (group_index + 1) * HD]
        scores = (
            jnp.einsum("thd,kd->htk", query_part, key_part, preferred_element_type=jnp.float32)
            * score_scale
        )
        scores = jnp.where(causal[None], scores, masked_score)
        top = jnp.max(scores, axis=-1, keepdims=True)
        summed = jnp.sum(jnp.exp(scores - top), axis=-1, keepdims=True)
        log_total = top + jnp.log(summed)
        probs = jnp.exp(scores - log_total)
        probs_low = probs.astype(jnp.bfloat16)
        context_part = jnp.einsum(
            "htk,kd->thd", probs_low, value_part, preferred_element_type=jnp.float32
        ).astype(jnp.bfloat16)
        dprobs = jnp.einsum(
            "thd,kd->htk", grad_part, value_part, preferred_element_type=jnp.float32
        )
        rowdot = jnp.sum(
            grad_part.astype(jnp.float32) * context_part.astype(jnp.float32), axis=-1
        ).transpose(1, 0)[:, :, None]
        dscores = (probs * (dprobs - rowdot) * score_scale).astype(jnp.bfloat16)
        query_list.append(
            jnp.einsum("htk,kd->thd", dscores, key_part, preferred_element_type=jnp.float32).astype(
                jnp.bfloat16
            )
        )
        key_terms.append(
            jnp.einsum("htk,thd->kd", dscores, query_part, preferred_element_type=jnp.float32)
        )
        value_terms.append(
            jnp.einsum("htk,thd->kd", probs_low, grad_part, preferred_element_type=jnp.float32)
        )
        context_list.append(context_part)
    context = jnp.stack(context_list, axis=1).reshape(tok_rows, queries.shape[1])
    query_grad = jnp.stack(query_list, axis=1).reshape(tok_rows, queries.shape[1])
    key_term = jnp.concatenate(key_terms, axis=1)
    value_term = jnp.concatenate(value_terms, axis=1)
    kv_width = key_term.shape[1]
    kv_term = jnp.concatenate([key_term, value_term], axis=1).astype(jnp.bfloat16)
    kv_parts = lax.all_to_all(
        kv_term.reshape(fsdp_size, tok_rows, 2 * kv_width), "fsdp", 0, 0, tiled=True
    )
    kv_total = jnp.sum(kv_parts.astype(jnp.float32), axis=0)
    key_sum = kv_total[:, :kv_width]
    value_total = kv_total[:, kv_width:]
    key_grad = key_sum.astype(jnp.bfloat16)
    value_grad = value_total.astype(jnp.bfloat16)
    product = lax.dot_general(
        tokens, value_grad, (((0,), (0,)), ((), ())), preferred_element_type=jnp.float32
    )
    weight_term = (product * proj_scale).astype(jnp.bfloat16)
    weight_parts = lax.all_to_all(
        weight_term.reshape(fsdp_size, weight_rows, weight_term.shape[1]), "fsdp", 0, 0, tiled=True
    )
    weight_grad = jnp.sum(weight_parts.astype(jnp.float32), axis=0)
    token_sum = lax.dot_general(
        value_grad,
        weight_all,
        (((1,), (1,)), ((), ())),
        preferred_element_type=jnp.float32,
    )
    token_grad = (token_sum * proj_scale).astype(jnp.bfloat16)
    replicas = lax.axis_size("replica")
    local_term = frag_local[0].astype(jnp.float32)
    own_sum = lax.psum_scatter(local_term, "replica", scatter_dimension=1, tiled=True)
    delta = frag_global - own_sum / replicas
    new_momentum = outer_momentum * frag_momentum + delta
    new_global = frag_global - outer_rate * (delta + outer_momentum * new_momentum)
    refreshed_local = lax.all_gather(new_global.astype(jnp.bfloat16), "replica", axis=1, tiled=True)
    return (
        context[None],
        query_grad[None],
        key_grad[None],
        weight_grad[None],
        token_grad[None],
        new_global,
        new_momentum,
        refreshed_local,
    )


def solution(mesh):
    return jax.shard_map(
        on_device,
        mesh=mesh,
        in_specs=(
            P("replica", "fsdp", None),
            P("replica", "fsdp", None),
            P("replica", "fsdp", None),
            P("fsdp", None),
            P("replica", "fsdp", None),
            P("fsdp", "replica"),
            P("fsdp", "replica"),
            P("replica", "fsdp", None),
        ),
        out_specs=(
            P("replica", "fsdp", None),
            P("replica", "fsdp", None),
            P("replica", "fsdp", None),
            P("replica", "fsdp", None),
            P("replica", "fsdp", None),
            P("fsdp", "replica"),
            P("fsdp", "replica"),
            P("fsdp", None),
        ),
        check_vma=False,
    )
```

```python
import jax
import jax.numpy as jnp
from jax import lax
from jax.sharding import PartitionSpec as P

HD = 128


outer_momentum = 0.9
outer_rate = 0.7
masked_score = -1e30


def on_device(
    tokens, queries, keys, value_weight, ctx_grad, frag_global, frag_momentum, frag_local
):
    tokens = tokens[0]
    queries = queries[0]
    keys = keys[0]
    ctx_grad = ctx_grad[0]
    tok_rows = tokens.shape[0]
    model_width = tokens.shape[1]
    proj_scale = model_width ** (-0.5)
    score_scale = HD ** (-0.5)
    kv_heads = keys.shape[1] // HD
    group = queries.shape[1] // (kv_heads * HD)
    key_rows = keys.shape[0]
    weight_rows = value_weight.shape[0]
    fsdp_size = lax.axis_size("fsdp")
    gathered = lax.all_gather(
        jnp.concatenate([keys, value_weight], axis=0), "fsdp", axis=0, tiled=False
    )
    keys_all = gathered[:, :key_rows].reshape(fsdp_size * key_rows, keys.shape[1])
    weight_all = gathered[:, key_rows:].reshape(fsdp_size * weight_rows, value_weight.shape[1])
    value_sum = jnp.dot(tokens, weight_all, preferred_element_type=jnp.float32)
    values = (value_sum * proj_scale).astype(jnp.bfloat16)
    values_all = lax.all_gather(values, "fsdp", axis=0, tiled=True)
    length_all = keys_all.shape[0]
    query_pos = lax.axis_index("fsdp") * tok_rows + jnp.arange(tok_rows)
    causal = jnp.arange(length_all)[None, :] <= query_pos[:, None]
    query_heads = queries.reshape(tok_rows, kv_heads, group, HD)
    grad_heads = ctx_grad.reshape(tok_rows, kv_heads, group, HD)
    context_list = []
    query_list = []
    key_terms = []
    value_terms = []
    for group_index in range(kv_heads):
        query_part = query_heads[:, group_index]
        grad_part = grad_heads[:, group_index]
        key_part = keys_all[:, group_index * HD : (group_index + 1) * HD]
        value_part = values_all[:, group_index * HD : (group_index + 1) * HD]
        scores = (
            jnp.einsum("thd,kd->htk", query_part, key_part, preferred_element_type=jnp.float32)
            * score_scale
        )
        scores = jnp.where(causal[None], scores, masked_score)
        top = jnp.max(scores, axis=-1, keepdims=True)
        summed = jnp.sum(jnp.exp(scores - top), axis=-1, keepdims=True)
        log_total = top + jnp.log(summed)
        probs = jnp.exp(scores - log_total)
        probs_low = probs.astype(jnp.bfloat16)
        context_part = jnp.einsum(
            "htk,kd->thd", probs_low, value_part, preferred_element_type=jnp.float32
        ).astype(jnp.bfloat16)
        dprobs = jnp.einsum(
            "thd,kd->htk", grad_part, value_part, preferred_element_type=jnp.float32
        )
        rowdot = jnp.sum(
            grad_part.astype(jnp.float32) * context_part.astype(jnp.float32), axis=-1
        ).transpose(1, 0)[:, :, None]
        dscores = (probs * (dprobs - rowdot) * score_scale).astype(jnp.bfloat16)
        query_list.append(
            jnp.einsum("htk,kd->thd", dscores, key_part, preferred_element_type=jnp.float32).astype(
                jnp.bfloat16
            )
        )
        key_terms.append(
            jnp.einsum("htk,thd->kd", dscores, query_part, preferred_element_type=jnp.float32)
        )
        value_terms.append(
            jnp.einsum("htk,thd->kd", probs_low, grad_part, preferred_element_type=jnp.float32)
        )
        context_list.append(context_part)
    context = jnp.stack(context_list, axis=1).reshape(tok_rows, queries.shape[1])
    query_grad = jnp.stack(query_list, axis=1).reshape(tok_rows, queries.shape[1])
    key_term = jnp.concatenate(key_terms, axis=1)
    value_term = jnp.concatenate(value_terms, axis=1)
    kv_width = key_term.shape[1]
    kv_term = jnp.concatenate([key_term, value_term], axis=1).astype(jnp.bfloat16)
    kv_parts = lax.all_to_all(
        kv_term.reshape(fsdp_size, tok_rows, 2 * kv_width), "fsdp", 0, 0, tiled=True
    )
    kv_total = jnp.sum(kv_parts.astype(jnp.float32), axis=0)
    key_sum = kv_total[:, :kv_width]
    value_total = kv_total[:, kv_width:]
    key_grad = key_sum.astype(jnp.bfloat16)
    value_grad = value_total.astype(jnp.bfloat16)
    product = lax.dot_general(
        tokens, value_grad, (((0,), (0,)), ((), ())), preferred_element_type=jnp.float32
    )
    weight_term = (product * proj_scale).astype(jnp.bfloat16)
    weight_parts = lax.all_to_all(
        weight_term.reshape(fsdp_size, weight_rows, weight_term.shape[1]), "fsdp", 0, 0, tiled=True
    )
    weight_grad = jnp.sum(weight_parts.astype(jnp.float32), axis=0)
    token_sum = lax.dot_general(
        value_grad,
        weight_all,
        (((1,), (1,)), ((), ())),
        preferred_element_type=jnp.float32,
    )
    token_grad = (token_sum * proj_scale).astype(jnp.bfloat16)
    replicas = lax.axis_size("replica")
    share_cols = frag_global.shape[1]
    frag_rows = frag_global.shape[0]
    local_parts = lax.all_to_all(
        frag_local[0].reshape(frag_rows, replicas, share_cols).transpose(1, 0, 2),
        "replica",
        0,
        0,
        tiled=True,
    )
    own_sum = jnp.sum(local_parts.astype(jnp.float32), axis=0)
    delta = frag_global - own_sum / replicas
    new_momentum = outer_momentum * frag_momentum + delta
    new_global = frag_global - outer_rate * (delta + outer_momentum * new_momentum)
    refreshed_parts = lax.all_to_all(
        jnp.broadcast_to(
            new_global.astype(jnp.bfloat16)[None], (replicas, frag_rows, share_cols)
        ),
        "replica",
        0,
        0,
        tiled=True,
    )
    refreshed_local = refreshed_parts.transpose(1, 0, 2).reshape(frag_rows, replicas * share_cols)
    return (
        context[None],
        query_grad[None],
        key_grad[None],
        weight_grad[None],
        token_grad[None],
        new_global,
        new_momentum,
        refreshed_local,
    )


def solution(mesh):
    return jax.shard_map(
        on_device,
        mesh=mesh,
        in_specs=(
            P("replica", "fsdp", None),
            P("replica", "fsdp", None),
            P("replica", "fsdp", None),
            P("fsdp", None),
            P("replica", "fsdp", None),
            P("fsdp", "replica"),
            P("fsdp", "replica"),
            P("replica", "fsdp", None),
        ),
        out_specs=(
            P("replica", "fsdp", None),
            P("replica", "fsdp", None),
            P("replica", "fsdp", None),
            P("replica", "fsdp", None),
            P("replica", "fsdp", None),
            P("fsdp", "replica"),
            P("fsdp", "replica"),
            P("fsdp", None),
        ),
        check_vma=False,
    )
```

```python
import jax
import jax.numpy as jnp
from jax import lax
from jax.sharding import PartitionSpec as P

HD = 128


outer_momentum = 0.9
outer_rate = 0.7
masked_score = -1e30


def on_device(
    tokens, queries, keys, value_weight, ctx_grad, frag_global, frag_momentum, frag_local
):
    tokens = tokens[0]
    queries = queries[0]
    keys = keys[0]
    ctx_grad = ctx_grad[0]
    tok_rows = tokens.shape[0]
    model_width = tokens.shape[1]
    proj_scale = model_width ** (-0.5)
    score_scale = HD ** (-0.5)
    kv_heads = keys.shape[1] // HD
    group = queries.shape[1] // (kv_heads * HD)
    key_rows = keys.shape[0]
    weight_rows = value_weight.shape[0]
    fsdp_size = lax.axis_size("fsdp")
    gathered = lax.all_gather(
        jnp.concatenate([keys, value_weight], axis=0), "fsdp", axis=0, tiled=False
    )
    keys_all = gathered[:, :key_rows].reshape(fsdp_size * key_rows, keys.shape[1])
    weight_all = gathered[:, key_rows:].reshape(fsdp_size * weight_rows, value_weight.shape[1])
    replicas = lax.axis_size("replica")
    share_cols = frag_global.shape[1]
    frag_rows = frag_global.shape[0]
    local_parts = lax.all_to_all(
        frag_local[0].reshape(frag_rows, replicas, share_cols).transpose(1, 0, 2),
        "replica",
        0,
        0,
        tiled=True,
    )
    own_sum = jnp.sum(local_parts.astype(jnp.float32), axis=0)
    delta = frag_global - own_sum / replicas
    new_momentum = outer_momentum * frag_momentum + delta
    new_global = frag_global - outer_rate * (delta + outer_momentum * new_momentum)
    refreshed_parts = lax.all_to_all(
        jnp.broadcast_to(
            new_global.astype(jnp.bfloat16)[None], (replicas, frag_rows, share_cols)
        ),
        "replica",
        0,
        0,
        tiled=True,
    )
    refreshed_local = refreshed_parts.transpose(1, 0, 2).reshape(frag_rows, replicas * share_cols)
    refreshed_local, keys_all = lax.optimization_barrier((refreshed_local, keys_all))
    value_sum = jnp.dot(tokens, weight_all, preferred_element_type=jnp.float32)
    values = (value_sum * proj_scale).astype(jnp.bfloat16)
    values_all = lax.all_gather(values, "fsdp", axis=0, tiled=True)
    length_all = keys_all.shape[0]
    query_pos = lax.axis_index("fsdp") * tok_rows + jnp.arange(tok_rows)
    causal = jnp.arange(length_all)[None, :] <= query_pos[:, None]
    query_heads = queries.reshape(tok_rows, kv_heads, group, HD)
    grad_heads = ctx_grad.reshape(tok_rows, kv_heads, group, HD)
    prob_list = []
    value_terms = []
    for group_index in range(kv_heads):
        query_part = query_heads[:, group_index]
        grad_part = grad_heads[:, group_index]
        key_part = keys_all[:, group_index * HD : (group_index + 1) * HD]
        scores = (
            jnp.einsum("thd,kd->htk", query_part, key_part, preferred_element_type=jnp.float32)
            * score_scale
        )
        scores = jnp.where(causal[None], scores, masked_score)
        top = jnp.max(scores, axis=-1, keepdims=True)
        summed = jnp.sum(jnp.exp(scores - top), axis=-1, keepdims=True)
        log_total = top + jnp.log(summed)
        probs = jnp.exp(scores - log_total)
        probs_low = probs.astype(jnp.bfloat16)
        prob_list.append(probs)
        value_terms.append(
            jnp.einsum("htk,thd->kd", probs_low, grad_part, preferred_element_type=jnp.float32)
        )
    value_term = jnp.concatenate(value_terms, axis=1).astype(jnp.bfloat16)
    value_term, values_all = lax.optimization_barrier((value_term, values_all))
    kv_width = value_term.shape[1]
    value_parts = lax.all_to_all(
        value_term.reshape(fsdp_size, tok_rows, kv_width), "fsdp", 0, 0, tiled=True
    )
    value_grad = jnp.sum(value_parts.astype(jnp.float32), axis=0).astype(jnp.bfloat16)
    context_list = []
    query_list = []
    key_terms = []
    for group_index in range(kv_heads):
        query_part = query_heads[:, group_index]
        grad_part = grad_heads[:, group_index]
        key_part = keys_all[:, group_index * HD : (group_index + 1) * HD]
        value_part = values_all[:, group_index * HD : (group_index + 1) * HD]
        probs = prob_list[group_index]
        probs_low = probs.astype(jnp.bfloat16)
        context_part = jnp.einsum(
            "htk,kd->thd", probs_low, value_part, preferred_element_type=jnp.float32
        ).astype(jnp.bfloat16)
        dprobs = jnp.einsum(
            "thd,kd->htk", grad_part, value_part, preferred_element_type=jnp.float32
        )
        rowdot = jnp.sum(
            grad_part.astype(jnp.float32) * context_part.astype(jnp.float32), axis=-1
        ).transpose(1, 0)[:, :, None]
        dscores = (probs * (dprobs - rowdot) * score_scale).astype(jnp.bfloat16)
        query_list.append(
            jnp.einsum("htk,kd->thd", dscores, key_part, preferred_element_type=jnp.float32).astype(
                jnp.bfloat16
            )
        )
        key_terms.append(
            jnp.einsum("htk,thd->kd", dscores, query_part, preferred_element_type=jnp.float32)
        )
        context_list.append(context_part)
    context = jnp.stack(context_list, axis=1).reshape(tok_rows, queries.shape[1])
    query_grad = jnp.stack(query_list, axis=1).reshape(tok_rows, queries.shape[1])
    key_term = jnp.concatenate(key_terms, axis=1).astype(jnp.bfloat16)
    key_parts = lax.all_to_all(
        key_term.reshape(fsdp_size, tok_rows, kv_width), "fsdp", 0, 0, tiled=True
    )
    key_grad = jnp.sum(key_parts.astype(jnp.float32), axis=0).astype(jnp.bfloat16)
    product = lax.dot_general(
        tokens, value_grad, (((0,), (0,)), ((), ())), preferred_element_type=jnp.float32
    )
    weight_term = (product * proj_scale).astype(jnp.bfloat16)
    weight_parts = lax.all_to_all(
        weight_term.reshape(fsdp_size, weight_rows, weight_term.shape[1]), "fsdp", 0, 0, tiled=True
    )
    weight_grad = jnp.sum(weight_parts.astype(jnp.float32), axis=0)
    token_sum = lax.dot_general(
        value_grad,
        weight_all,
        (((1,), (1,)), ((), ())),
        preferred_element_type=jnp.float32,
    )
    token_grad = (token_sum * proj_scale).astype(jnp.bfloat16)
    return (
        context[None],
        query_grad[None],
        key_grad[None],
        weight_grad[None],
        token_grad[None],
        new_global,
        new_momentum,
        refreshed_local,
    )


def solution(mesh):
    return jax.shard_map(
        on_device,
        mesh=mesh,
        in_specs=(
            P("replica", "fsdp", None),
            P("replica", "fsdp", None),
            P("replica", "fsdp", None),
            P("fsdp", None),
            P("replica", "fsdp", None),
            P("fsdp", "replica"),
            P("fsdp", "replica"),
            P("replica", "fsdp", None),
        ),
        out_specs=(
            P("replica", "fsdp", None),
            P("replica", "fsdp", None),
            P("replica", "fsdp", None),
            P("replica", "fsdp", None),
            P("replica", "fsdp", None),
            P("fsdp", "replica"),
            P("fsdp", "replica"),
            P("fsdp", None),
        ),
        check_vma=False,
    )
```

```python
import jax
import jax.numpy as jnp
from jax import lax
from jax.sharding import PartitionSpec as P

HD = 128


outer_momentum = 0.9
outer_rate = 0.7
masked_score = -1e30


def on_device(
    tokens, queries, keys, value_weight, ctx_grad, frag_global, frag_momentum, frag_local
):
    tokens = tokens[0]
    queries = queries[0]
    keys = keys[0]
    ctx_grad = ctx_grad[0]
    tok_rows = tokens.shape[0]
    model_width = tokens.shape[1]
    proj_scale = model_width ** (-0.5)
    score_scale = HD ** (-0.5)
    kv_heads = keys.shape[1] // HD
    group = queries.shape[1] // (kv_heads * HD)
    key_rows = keys.shape[0]
    weight_rows = value_weight.shape[0]
    planes = lax.axis_size("yhi")
    inner = lax.axis_size("xc")
    plane = lax.axis_index("yhi")
    spot = lax.axis_index("xc")
    core = spot % 2
    swap = [(0, 1), (1, 0)]
    up = [(0, 1)]
    down = [(1, 0)]
    pair = [(j, j ^ 1) for j in range(inner)]

    def across(rows, perm):
        half = rows.shape[0] // 2
        mine = lax.dynamic_slice_in_dim(rows, core * half, half, 0)
        got = lax.ppermute(mine, "yhi", perm)
        other = lax.ppermute(got, "xc", pair)
        return jnp.where(
            core == 0, jnp.concatenate([got, other], 0), jnp.concatenate([other, got], 0)
        )

    def by_plane(own, far):
        return jnp.where(
            plane == 0, jnp.concatenate([own, far], 0), jnp.concatenate([far, own], 0)
        )

    def reduce_rows(term, block):
        width = term.shape[1]
        parts = lax.all_to_all(
            term.reshape(planes, inner, block, width), "xc", 1, 1, tiled=True
        )
        return jnp.sum(parts.astype(jnp.float32), axis=1)

    plane_rows = lax.all_gather(
        jnp.concatenate([keys, value_weight], axis=0), "xc", axis=0, tiled=False
    )
    plane_keys = plane_rows[:, :key_rows].reshape(inner * key_rows, keys.shape[1])
    plane_weight = plane_rows[:, key_rows:].reshape(inner * weight_rows, value_weight.shape[1])
    weight_all = by_plane(plane_weight, across(plane_weight, swap))
    early_keys = across(plane_keys, up)
    keys_all = jnp.concatenate([jnp.where(plane == 0, plane_keys, early_keys), plane_keys], 0)
    replicas = lax.axis_size("replica")
    share_cols = frag_global.shape[1]
    frag_rows = frag_global.shape[0]
    local_parts = lax.all_to_all(
        frag_local[0].reshape(frag_rows, replicas, share_cols).transpose(1, 0, 2),
        "replica",
        0,
        0,
        tiled=True,
    )
    own_sum = jnp.sum(local_parts.astype(jnp.float32), axis=0)
    delta = frag_global - own_sum / replicas
    new_momentum = outer_momentum * frag_momentum + delta
    new_global = frag_global - outer_rate * (delta + outer_momentum * new_momentum)
    refreshed_parts = lax.all_to_all(
        jnp.broadcast_to(
            new_global.astype(jnp.bfloat16)[None], (replicas, frag_rows, share_cols)
        ),
        "replica",
        0,
        0,
        tiled=True,
    )
    refreshed_local = refreshed_parts.transpose(1, 0, 2).reshape(frag_rows, replicas * share_cols)
    refreshed_local, keys_all = lax.optimization_barrier((refreshed_local, keys_all))
    value_sum = jnp.dot(tokens, weight_all, preferred_element_type=jnp.float32)
    values = (value_sum * proj_scale).astype(jnp.bfloat16)
    plane_values = lax.all_gather(values, "xc", axis=0, tiled=True)
    early_values = across(plane_values, up)
    values_all = jnp.concatenate(
        [jnp.where(plane == 0, plane_values, early_values), plane_values], 0
    )
    length_all = keys_all.shape[0]
    query_pos = (plane * inner + spot) * tok_rows + jnp.arange(tok_rows)
    causal = jnp.arange(length_all)[None, :] <= query_pos[:, None]
    query_heads = queries.reshape(tok_rows, kv_heads, group, HD)
    grad_heads = ctx_grad.reshape(tok_rows, kv_heads, group, HD)
    prob_list = []
    value_terms = []
    for group_index in range(kv_heads):
        query_part = query_heads[:, group_index]
        grad_part = grad_heads[:, group_index]
        key_part = keys_all[:, group_index * HD : (group_index + 1) * HD]
        scores = (
            jnp.einsum("thd,kd->htk", query_part, key_part, preferred_element_type=jnp.float32)
            * score_scale
        )
        scores = jnp.where(causal[None], scores, masked_score)
        top = jnp.max(scores, axis=-1, keepdims=True)
        summed = jnp.sum(jnp.exp(scores - top), axis=-1, keepdims=True)
        log_total = top + jnp.log(summed)
        probs = jnp.exp(scores - log_total)
        probs_low = probs.astype(jnp.bfloat16)
        prob_list.append(probs)
        value_terms.append(
            jnp.einsum("htk,thd->kd", probs_low, grad_part, preferred_element_type=jnp.float32)
        )
    value_term = jnp.concatenate(value_terms, axis=1).astype(jnp.bfloat16)
    value_term, values_all = lax.optimization_barrier((value_term, values_all))
    kv_width = value_term.shape[1]
    value_sums = reduce_rows(value_term, tok_rows)
    value_late = lax.ppermute(value_sums[0], "yhi", down)
    value_grad = jnp.where(plane == 0, value_sums[0] + value_late, value_sums[1]).astype(
        jnp.bfloat16
    )
    context_list = []
    query_list = []
    key_terms = []
    for group_index in range(kv_heads):
        query_part = query_heads[:, group_index]
        grad_part = grad_heads[:, group_index]
        key_part = keys_all[:, group_index * HD : (group_index + 1) * HD]
        value_part = values_all[:, group_index * HD : (group_index + 1) * HD]
        probs = prob_list[group_index]
        probs_low = probs.astype(jnp.bfloat16)
        context_part = jnp.einsum(
            "htk,kd->thd", probs_low, value_part, preferred_element_type=jnp.float32
        ).astype(jnp.bfloat16)
        dprobs = jnp.einsum(
            "thd,kd->htk", grad_part, value_part, preferred_element_type=jnp.float32
        )
        rowdot = jnp.sum(
            grad_part.astype(jnp.float32) * context_part.astype(jnp.float32), axis=-1
        ).transpose(1, 0)[:, :, None]
        dscores = (probs * (dprobs - rowdot) * score_scale).astype(jnp.bfloat16)
        query_list.append(
            jnp.einsum("htk,kd->thd", dscores, key_part, preferred_element_type=jnp.float32).astype(
                jnp.bfloat16
            )
        )
        key_terms.append(
            jnp.einsum("htk,thd->kd", dscores, query_part, preferred_element_type=jnp.float32)
        )
        context_list.append(context_part)
    context = jnp.stack(context_list, axis=1).reshape(tok_rows, queries.shape[1])
    query_grad = jnp.stack(query_list, axis=1).reshape(tok_rows, queries.shape[1])
    key_term = jnp.concatenate(key_terms, axis=1).astype(jnp.bfloat16)
    key_sums = reduce_rows(key_term, tok_rows)
    key_late = lax.ppermute(key_sums[0], "yhi", down)
    key_grad = jnp.where(plane == 0, key_sums[0] + key_late, key_sums[1]).astype(jnp.bfloat16)
    product = lax.dot_general(
        tokens, value_grad, (((0,), (0,)), ((), ())), preferred_element_type=jnp.float32
    )
    weight_term = (product * proj_scale).astype(jnp.bfloat16)
    weight_sums = reduce_rows(weight_term, weight_rows)
    weight_own = lax.dynamic_index_in_dim(weight_sums, plane, 0, keepdims=False)
    weight_far = lax.dynamic_index_in_dim(weight_sums, planes - 1 - plane, 0, keepdims=False)
    weight_grad = weight_own + lax.ppermute(weight_far, "yhi", swap)
    token_sum = lax.dot_general(
        value_grad,
        weight_all,
        (((1,), (1,)), ((), ())),
        preferred_element_type=jnp.float32,
    )
    token_grad = (token_sum * proj_scale).astype(jnp.bfloat16)
    return (
        context[None],
        query_grad[None],
        key_grad[None],
        weight_grad[None],
        token_grad[None],
        new_global,
        new_momentum,
        refreshed_local,
    )


def solution(mesh):
    fsdp_size = mesh.shape["fsdp"]
    planes = 2
    split_mesh = jax.sharding.Mesh(
        mesh.devices.reshape(mesh.shape["replica"], planes, fsdp_size // planes),
        ("replica", "yhi", "xc"),
    )
    rows = ("yhi", "xc")
    return jax.shard_map(
        on_device,
        mesh=split_mesh,
        in_specs=(
            P("replica", rows, None),
            P("replica", rows, None),
            P("replica", rows, None),
            P(rows, None),
            P("replica", rows, None),
            P(rows, "replica"),
            P(rows, "replica"),
            P("replica", rows, None),
        ),
        out_specs=(
            P("replica", rows, None),
            P("replica", rows, None),
            P("replica", rows, None),
            P("replica", rows, None),
            P("replica", rows, None),
            P(rows, "replica"),
            P(rows, "replica"),
            P(rows, None),
        ),
        check_vma=False,
    )
```

```python
import jax
import jax.numpy as jnp
from jax import lax
from jax.sharding import PartitionSpec as P

HD = 128


outer_momentum = 0.9
outer_rate = 0.7
masked_score = -1e30


def on_device(
    tokens, queries, keys, value_weight, ctx_grad, frag_global, frag_momentum, frag_local
):
    tokens = tokens[0]
    queries = queries[0]
    keys = keys[0]
    ctx_grad = ctx_grad[0]
    tok_rows = tokens.shape[0]
    model_width = tokens.shape[1]
    proj_scale = model_width ** (-0.5)
    score_scale = HD ** (-0.5)
    kv_heads = keys.shape[1] // HD
    group = queries.shape[1] // (kv_heads * HD)
    key_rows = keys.shape[0]
    weight_rows = value_weight.shape[0]
    fsdp_size = lax.axis_size("fsdp")
    gathered = lax.all_gather(
        jnp.concatenate([keys, value_weight], axis=0), "fsdp", axis=0, tiled=False
    )
    keys_all = gathered[:, :key_rows].reshape(fsdp_size * key_rows, keys.shape[1])
    weight_all = gathered[:, key_rows:].reshape(fsdp_size * weight_rows, value_weight.shape[1])
    replicas = lax.axis_size("replica")
    share_cols = frag_global.shape[1]
    frag_rows = frag_global.shape[0]
    local_parts = lax.all_to_all(
        frag_local[0].reshape(frag_rows, replicas, share_cols).transpose(1, 0, 2),
        "replica",
        0,
        0,
        tiled=True,
    )
    own_sum = jnp.sum(local_parts.astype(jnp.float32), axis=0)
    delta = frag_global - own_sum / replicas
    new_momentum = outer_momentum * frag_momentum + delta
    new_global = frag_global - outer_rate * (delta + outer_momentum * new_momentum)
    refreshed_parts = lax.all_to_all(
        jnp.broadcast_to(
            new_global.astype(jnp.bfloat16)[None], (replicas, frag_rows, share_cols)
        ),
        "replica",
        0,
        0,
        tiled=True,
    )
    refreshed_local = refreshed_parts.transpose(1, 0, 2).reshape(frag_rows, replicas * share_cols)
    refreshed_local, keys_all = lax.optimization_barrier((refreshed_local, keys_all))
    value_sum = jnp.dot(tokens, weight_all, preferred_element_type=jnp.float32)
    values = (value_sum * proj_scale).astype(jnp.bfloat16)
    values_all = lax.all_gather(values, "fsdp", axis=0, tiled=True)
    length_all = keys_all.shape[0]
    query_pos = lax.axis_index("fsdp") * tok_rows + jnp.arange(tok_rows)
    causal = jnp.arange(length_all)[None, :] <= query_pos[:, None]
    query_heads = queries.reshape(tok_rows, kv_heads, group, HD)
    grad_heads = ctx_grad.reshape(tok_rows, kv_heads, group, HD)
    prob_list = []
    value_terms = []
    for group_index in range(kv_heads):
        query_part = query_heads[:, group_index]
        grad_part = grad_heads[:, group_index]
        key_part = keys_all[:, group_index * HD : (group_index + 1) * HD]
        scores = (
            jnp.einsum("thd,kd->htk", query_part, key_part, preferred_element_type=jnp.float32)
            * score_scale
        )
        scores = jnp.where(causal[None], scores, masked_score)
        top = jnp.max(scores, axis=-1, keepdims=True)
        summed = jnp.sum(jnp.exp(scores - top), axis=-1, keepdims=True)
        log_total = top + jnp.log(summed)
        probs = jnp.exp(scores - log_total)
        probs_low = probs.astype(jnp.bfloat16)
        prob_list.append(probs)
        value_terms.append(
            jnp.einsum("htk,thd->kd", probs_low, grad_part, preferred_element_type=jnp.float32)
        )
    value_term = jnp.concatenate(value_terms, axis=1).astype(jnp.bfloat16)
    value_term, values_all = lax.optimization_barrier((value_term, values_all))
    kv_width = value_term.shape[1]
    value_parts = lax.all_to_all(
        value_term.reshape(fsdp_size, tok_rows, kv_width), "fsdp", 0, 0, tiled=True
    )
    value_grad = jnp.sum(value_parts.astype(jnp.float32), axis=0).astype(jnp.bfloat16)
    context_list = []
    query_list = []
    key_terms = []
    for group_index in range(kv_heads):
        query_part = query_heads[:, group_index]
        grad_part = grad_heads[:, group_index]
        key_part = keys_all[:, group_index * HD : (group_index + 1) * HD]
        value_part = values_all[:, group_index * HD : (group_index + 1) * HD]
        probs = prob_list[group_index]
        probs_low = probs.astype(jnp.bfloat16)
        context_part = jnp.einsum(
            "htk,kd->thd", probs_low, value_part, preferred_element_type=jnp.float32
        ).astype(jnp.bfloat16)
        dprobs = jnp.einsum(
            "thd,kd->htk", grad_part, value_part, preferred_element_type=jnp.float32
        )
        rowdot = jnp.sum(
            grad_part.astype(jnp.float32) * context_part.astype(jnp.float32), axis=-1
        ).transpose(1, 0)[:, :, None]
        dscores = (probs * (dprobs - rowdot) * score_scale).astype(jnp.bfloat16)
        query_list.append(
            jnp.einsum("htk,kd->thd", dscores, key_part, preferred_element_type=jnp.float32).astype(
                jnp.bfloat16
            )
        )
        key_terms.append(
            jnp.einsum("htk,thd->kd", dscores, query_part, preferred_element_type=jnp.float32)
        )
        context_list.append(context_part)
    context = jnp.stack(context_list, axis=1).reshape(tok_rows, queries.shape[1])
    query_grad = jnp.stack(query_list, axis=1).reshape(tok_rows, queries.shape[1])
    key_term = jnp.concatenate(key_terms, axis=1).astype(jnp.bfloat16)
    key_parts = lax.all_to_all(
        key_term.reshape(fsdp_size, tok_rows, kv_width), "fsdp", 0, 0, tiled=True
    )
    key_grad = jnp.sum(key_parts.astype(jnp.float32), axis=0).astype(jnp.bfloat16)
    product = lax.dot_general(
        tokens, value_grad, (((0,), (0,)), ((), ())), preferred_element_type=jnp.float32
    )
    weight_term = (product * proj_scale).astype(jnp.bfloat16)
    weight_grad = lax.psum_scatter(
        weight_term, "fsdp", scatter_dimension=0, tiled=True
    ).astype(jnp.float32)
    token_sum = lax.dot_general(
        value_grad,
        weight_all,
        (((1,), (1,)), ((), ())),
        preferred_element_type=jnp.float32,
    )
    token_grad = (token_sum * proj_scale).astype(jnp.bfloat16)
    return (
        context[None],
        query_grad[None],
        key_grad[None],
        weight_grad[None],
        token_grad[None],
        new_global,
        new_momentum,
        refreshed_local,
    )


def solution(mesh):
    return jax.shard_map(
        on_device,
        mesh=mesh,
        in_specs=(
            P("replica", "fsdp", None),
            P("replica", "fsdp", None),
            P("replica", "fsdp", None),
            P("fsdp", None),
            P("replica", "fsdp", None),
            P("fsdp", "replica"),
            P("fsdp", "replica"),
            P("replica", "fsdp", None),
        ),
        out_specs=(
            P("replica", "fsdp", None),
            P("replica", "fsdp", None),
            P("replica", "fsdp", None),
            P("replica", "fsdp", None),
            P("replica", "fsdp", None),
            P("fsdp", "replica"),
            P("fsdp", "replica"),
            P("fsdp", None),
        ),
        check_vma=False,
    )
```

```python
import jax
import jax.numpy as jnp
from jax import lax
from jax.sharding import PartitionSpec as P

HD = 128


outer_momentum = 0.9
outer_rate = 0.7
masked_score = -1e30


def on_device(
    tokens, queries, keys, value_weight, ctx_grad, frag_global, frag_momentum, frag_local
):
    tokens = tokens[0]
    queries = queries[0]
    keys = keys[0]
    ctx_grad = ctx_grad[0]
    tok_rows = tokens.shape[0]
    model_width = tokens.shape[1]
    proj_scale = model_width ** (-0.5)
    score_scale = HD ** (-0.5)
    kv_heads = keys.shape[1] // HD
    group = queries.shape[1] // (kv_heads * HD)
    key_rows = keys.shape[0]
    weight_rows = value_weight.shape[0]
    fsdp_size = lax.axis_size("fsdp")
    gathered = lax.all_gather(
        jnp.concatenate([keys, value_weight], axis=0), "fsdp", axis=0, tiled=False
    )
    keys_all = gathered[:, :key_rows].reshape(fsdp_size * key_rows, keys.shape[1])
    weight_all = gathered[:, key_rows:].reshape(fsdp_size * weight_rows, value_weight.shape[1])
    replicas = lax.axis_size("replica")
    share_cols = frag_global.shape[1]
    frag_rows = frag_global.shape[0]
    local_parts = lax.all_to_all(
        frag_local[0].reshape(frag_rows, replicas, share_cols).transpose(1, 0, 2),
        "replica",
        0,
        0,
        tiled=True,
    )
    own_sum = jnp.sum(local_parts.astype(jnp.float32), axis=0)
    delta = frag_global - own_sum / replicas
    new_momentum = outer_momentum * frag_momentum + delta
    new_global = frag_global - outer_rate * (delta + outer_momentum * new_momentum)
    refreshed_parts = lax.all_to_all(
        jnp.broadcast_to(
            new_global.astype(jnp.bfloat16)[None], (replicas, frag_rows, share_cols)
        ),
        "replica",
        0,
        0,
        tiled=True,
    )
    refreshed_local = refreshed_parts.transpose(1, 0, 2).reshape(frag_rows, replicas * share_cols)
    refreshed_local, keys_all = lax.optimization_barrier((refreshed_local, keys_all))
    value_sum = jnp.dot(tokens, weight_all, preferred_element_type=jnp.float32)
    values = (value_sum * proj_scale).astype(jnp.bfloat16)
    values_all = lax.all_gather(values, "fsdp", axis=0, tiled=True)
    length_all = keys_all.shape[0]
    query_pos = lax.axis_index("fsdp") * tok_rows + jnp.arange(tok_rows)
    causal = jnp.arange(length_all)[None, :] <= query_pos[:, None]
    query_heads = queries.reshape(tok_rows, kv_heads, group, HD)
    grad_heads = ctx_grad.reshape(tok_rows, kv_heads, group, HD)
    key_groups = keys_all.reshape(length_all, kv_heads, HD)
    scores = (
        jnp.einsum("tghd,sgd->ghts", query_heads, key_groups, preferred_element_type=jnp.float32)
        * score_scale
    )
    scores = jnp.where(causal[None, None], scores, masked_score)
    top = jnp.max(scores, axis=-1, keepdims=True)
    summed = jnp.sum(jnp.exp(scores - top), axis=-1, keepdims=True)
    log_total = top + jnp.log(summed)
    probs = jnp.exp(scores - log_total)
    probs_low = probs.astype(jnp.bfloat16)
    value_term = (
        jnp.einsum("ghts,tghd->sgd", probs_low, grad_heads, preferred_element_type=jnp.float32)
        .reshape(length_all, kv_heads * HD)
        .astype(jnp.bfloat16)
    )
    value_term, values_all = lax.optimization_barrier((value_term, values_all))
    kv_width = value_term.shape[1]
    value_parts = lax.all_to_all(
        value_term.reshape(fsdp_size, tok_rows, kv_width), "fsdp", 0, 0, tiled=True
    )
    value_grad = jnp.sum(value_parts.astype(jnp.float32), axis=0).astype(jnp.bfloat16)
    value_groups = values_all.reshape(length_all, kv_heads, HD)
    context_heads = jnp.einsum(
        "ghts,sgd->tghd", probs_low, value_groups, preferred_element_type=jnp.float32
    ).astype(jnp.bfloat16)
    dprobs = jnp.einsum(
        "tghd,sgd->ghts", grad_heads, value_groups, preferred_element_type=jnp.float32
    )
    rowdot = jnp.sum(
        grad_heads.astype(jnp.float32) * context_heads.astype(jnp.float32), axis=-1
    ).transpose(1, 2, 0)[..., None]
    dscores = (probs * (dprobs - rowdot) * score_scale).astype(jnp.bfloat16)
    query_grad = (
        jnp.einsum("ghts,sgd->tghd", dscores, key_groups, preferred_element_type=jnp.float32)
        .astype(jnp.bfloat16)
        .reshape(tok_rows, queries.shape[1])
    )
    key_term = (
        jnp.einsum("ghts,tghd->sgd", dscores, query_heads, preferred_element_type=jnp.float32)
        .reshape(length_all, kv_width)
        .astype(jnp.bfloat16)
    )
    context = context_heads.reshape(tok_rows, queries.shape[1])
    key_parts = lax.all_to_all(
        key_term.reshape(fsdp_size, tok_rows, kv_width), "fsdp", 0, 0, tiled=True
    )
    key_grad = jnp.sum(key_parts.astype(jnp.float32), axis=0).astype(jnp.bfloat16)
    product = lax.dot_general(
        tokens, value_grad, (((0,), (0,)), ((), ())), preferred_element_type=jnp.float32
    )
    weight_term = (product * proj_scale).astype(jnp.bfloat16)
    weight_grad = lax.psum_scatter(
        weight_term, "fsdp", scatter_dimension=0, tiled=True
    ).astype(jnp.float32)
    token_sum = lax.dot_general(
        value_grad,
        weight_all,
        (((1,), (1,)), ((), ())),
        preferred_element_type=jnp.float32,
    )
    token_grad = (token_sum * proj_scale).astype(jnp.bfloat16)
    return (
        context[None],
        query_grad[None],
        key_grad[None],
        weight_grad[None],
        token_grad[None],
        new_global,
        new_momentum,
        refreshed_local,
    )


def solution(mesh):
    return jax.shard_map(
        on_device,
        mesh=mesh,
        in_specs=(
            P("replica", "fsdp", None),
            P("replica", "fsdp", None),
            P("replica", "fsdp", None),
            P("fsdp", None),
            P("replica", "fsdp", None),
            P("fsdp", "replica"),
            P("fsdp", "replica"),
            P("replica", "fsdp", None),
        ),
        out_specs=(
            P("replica", "fsdp", None),
            P("replica", "fsdp", None),
            P("replica", "fsdp", None),
            P("replica", "fsdp", None),
            P("replica", "fsdp", None),
            P("fsdp", "replica"),
            P("fsdp", "replica"),
            P("fsdp", None),
        ),
        check_vma=False,
    )
```

```python
import jax
import jax.numpy as jnp
from jax import lax
from jax.sharding import PartitionSpec as P

HD = 128


outer_momentum = 0.9
outer_rate = 0.7
masked_score = -1e30


def on_device(
    tokens, queries, keys, value_weight, ctx_grad, frag_global, frag_momentum, frag_local
):
    tokens = tokens[0]
    queries = queries[0]
    keys = keys[0]
    ctx_grad = ctx_grad[0]
    tok_rows = tokens.shape[0]
    model_width = tokens.shape[1]
    proj_scale = model_width ** (-0.5)
    score_scale = HD ** (-0.5)
    kv_heads = keys.shape[1] // HD
    group = queries.shape[1] // (kv_heads * HD)
    key_rows = keys.shape[0]
    weight_rows = value_weight.shape[0]
    fsdp_size = lax.axis_size("fsdp")
    gathered = lax.all_gather(
        jnp.concatenate([keys, value_weight], axis=0), "fsdp", axis=0, tiled=False
    )
    keys_all = gathered[:, :key_rows].reshape(fsdp_size * key_rows, keys.shape[1])
    weight_all = gathered[:, key_rows:].reshape(fsdp_size * weight_rows, value_weight.shape[1])
    replicas = lax.axis_size("replica")
    share_cols = frag_global.shape[1]
    frag_rows = frag_global.shape[0]
    local_parts = lax.all_to_all(
        frag_local[0].reshape(frag_rows, replicas, share_cols).transpose(1, 0, 2),
        "replica",
        0,
        0,
        tiled=True,
    )
    own_sum = jnp.sum(local_parts.astype(jnp.float32), axis=0)
    delta = frag_global - own_sum / replicas
    new_momentum = outer_momentum * frag_momentum + delta
    new_global = frag_global - outer_rate * (delta + outer_momentum * new_momentum)
    refreshed_parts = lax.all_to_all(
        jnp.broadcast_to(
            new_global.astype(jnp.bfloat16)[None], (replicas, frag_rows, share_cols)
        ),
        "replica",
        0,
        0,
        tiled=True,
    )
    refreshed_local = refreshed_parts.transpose(1, 0, 2).reshape(frag_rows, replicas * share_cols)
    refreshed_local, keys_all = lax.optimization_barrier((refreshed_local, keys_all))
    value_sum = jnp.dot(tokens, weight_all, preferred_element_type=jnp.float32)
    values = (value_sum * proj_scale).astype(jnp.bfloat16)
    values_all = lax.all_gather(values, "fsdp", axis=0, tiled=True)
    length_all = keys_all.shape[0]
    query_pos = lax.axis_index("fsdp") * tok_rows + jnp.arange(tok_rows)
    causal = jnp.arange(length_all)[None, :] <= query_pos[:, None]
    query_heads = queries.reshape(tok_rows, kv_heads, group, HD)
    grad_heads = ctx_grad.reshape(tok_rows, kv_heads, group, HD)
    key_groups = keys_all.reshape(length_all, kv_heads, HD)
    scores = (
        jnp.einsum("tghd,sgd->ghts", query_heads, key_groups, preferred_element_type=jnp.float32)
        * score_scale
    )
    scores = jnp.where(causal[None, None], scores, masked_score)
    top = jnp.max(scores, axis=-1, keepdims=True)
    summed = jnp.sum(jnp.exp(scores - top), axis=-1, keepdims=True)
    log_total = top + jnp.log(summed)
    probs = jnp.exp(scores - log_total)
    probs_low = probs.astype(jnp.bfloat16)
    value_term = (
        jnp.einsum("ghts,tghd->sgd", probs_low, grad_heads, preferred_element_type=jnp.float32)
        .reshape(length_all, kv_heads * HD)
        .astype(jnp.bfloat16)
    )
    kv_width = value_term.shape[1]
    value_parts = lax.all_to_all(
        value_term.reshape(fsdp_size, tok_rows, kv_width), "fsdp", 0, 0, tiled=True
    )
    value_grad = jnp.sum(value_parts.astype(jnp.float32), axis=0).astype(jnp.bfloat16)
    value_groups = values_all.reshape(length_all, kv_heads, HD)
    context_heads = jnp.einsum(
        "ghts,sgd->tghd", probs_low, value_groups, preferred_element_type=jnp.float32
    ).astype(jnp.bfloat16)
    dprobs = jnp.einsum(
        "tghd,sgd->ghts", grad_heads, value_groups, preferred_element_type=jnp.float32
    )
    rowdot = jnp.sum(
        grad_heads.astype(jnp.float32) * context_heads.astype(jnp.float32), axis=-1
    ).transpose(1, 2, 0)[..., None]
    dscores = (probs * (dprobs - rowdot) * score_scale).astype(jnp.bfloat16)
    query_grad = (
        jnp.einsum("ghts,sgd->tghd", dscores, key_groups, preferred_element_type=jnp.float32)
        .astype(jnp.bfloat16)
        .reshape(tok_rows, queries.shape[1])
    )
    key_term = (
        jnp.einsum("ghts,tghd->sgd", dscores, query_heads, preferred_element_type=jnp.float32)
        .reshape(length_all, kv_width)
        .astype(jnp.bfloat16)
    )
    context = context_heads.reshape(tok_rows, queries.shape[1])
    key_term, token_source = lax.optimization_barrier((key_term, value_grad))
    key_parts = lax.all_to_all(
        key_term.reshape(fsdp_size, tok_rows, kv_width), "fsdp", 0, 0, tiled=True
    )
    key_grad = jnp.sum(key_parts.astype(jnp.float32), axis=0).astype(jnp.bfloat16)
    product = lax.dot_general(
        tokens, value_grad, (((0,), (0,)), ((), ())), preferred_element_type=jnp.float32
    )
    weight_term = (product * proj_scale).astype(jnp.bfloat16)
    weight_grad = lax.psum_scatter(
        weight_term, "fsdp", scatter_dimension=0, tiled=True
    ).astype(jnp.float32)
    token_sum = lax.dot_general(
        token_source,
        weight_all,
        (((1,), (1,)), ((), ())),
        preferred_element_type=jnp.float32,
    )
    token_grad = (token_sum * proj_scale).astype(jnp.bfloat16)
    return (
        context[None],
        query_grad[None],
        key_grad[None],
        weight_grad[None],
        token_grad[None],
        new_global,
        new_momentum,
        refreshed_local,
    )


def solution(mesh):
    return jax.shard_map(
        on_device,
        mesh=mesh,
        in_specs=(
            P("replica", "fsdp", None),
            P("replica", "fsdp", None),
            P("replica", "fsdp", None),
            P("fsdp", None),
            P("replica", "fsdp", None),
            P("fsdp", "replica"),
            P("fsdp", "replica"),
            P("replica", "fsdp", None),
        ),
        out_specs=(
            P("replica", "fsdp", None),
            P("replica", "fsdp", None),
            P("replica", "fsdp", None),
            P("replica", "fsdp", None),
            P("replica", "fsdp", None),
            P("fsdp", "replica"),
            P("fsdp", "replica"),
            P("fsdp", None),
        ),
        check_vma=False,
    )
```

```python
import jax
import jax.numpy as jnp
from jax import lax
from jax.sharding import PartitionSpec as P

HD = 128


outer_momentum = 0.9
outer_rate = 0.7
masked_score = -1e30


def on_device(
    tokens, queries, keys, value_weight, ctx_grad, frag_global, frag_momentum, frag_local
):
    tokens = tokens[0]
    queries = queries[0]
    keys = keys[0]
    ctx_grad = ctx_grad[0]
    tok_rows = tokens.shape[0]
    model_width = tokens.shape[1]
    proj_scale = model_width ** (-0.5)
    score_scale = HD ** (-0.5)
    kv_heads = keys.shape[1] // HD
    group = queries.shape[1] // (kv_heads * HD)
    key_rows = keys.shape[0]
    weight_rows = value_weight.shape[0]
    fsdp_size = lax.axis_size("fsdp")
    gathered = lax.all_gather(
        jnp.concatenate([keys, value_weight], axis=0), "fsdp", axis=0, tiled=False
    )
    keys_all = gathered[:, :key_rows].reshape(fsdp_size * key_rows, keys.shape[1])
    weight_all = gathered[:, key_rows:].reshape(fsdp_size * weight_rows, value_weight.shape[1])
    value_sum = jnp.dot(tokens, weight_all, preferred_element_type=jnp.float32)
    values = (value_sum * proj_scale).astype(jnp.bfloat16)
    values_all = lax.all_gather(values, "fsdp", axis=0, tiled=True)
    length_all = keys_all.shape[0]
    query_pos = lax.axis_index("fsdp") * tok_rows + jnp.arange(tok_rows)
    causal = jnp.arange(length_all)[None, :] <= query_pos[:, None]
    query_heads = queries.reshape(tok_rows, kv_heads, group, HD)
    grad_heads = ctx_grad.reshape(tok_rows, kv_heads, group, HD)
    key_groups = keys_all.reshape(length_all, kv_heads, HD)
    scores = (
        jnp.einsum("tghd,sgd->ghts", query_heads, key_groups, preferred_element_type=jnp.float32)
        * score_scale
    )
    scores = jnp.where(causal[None, None], scores, masked_score)
    top = jnp.max(scores, axis=-1, keepdims=True)
    summed = jnp.sum(jnp.exp(scores - top), axis=-1, keepdims=True)
    log_total = top + jnp.log(summed)
    probs = jnp.exp(scores - log_total)
    probs_low = probs.astype(jnp.bfloat16)
    value_term = (
        jnp.einsum("ghts,tghd->sgd", probs_low, grad_heads, preferred_element_type=jnp.float32)
        .reshape(length_all, kv_heads * HD)
        .astype(jnp.bfloat16)
    )
    kv_width = value_term.shape[1]
    value_parts = lax.all_to_all(
        value_term.reshape(fsdp_size, tok_rows, kv_width), "fsdp", 0, 0, tiled=True
    )
    value_grad = jnp.sum(value_parts.astype(jnp.float32), axis=0).astype(jnp.bfloat16)
    late_local, value_grad = lax.optimization_barrier((frag_local, value_grad))
    replicas = lax.axis_size("replica")
    share_cols = frag_global.shape[1]
    frag_rows = frag_global.shape[0]
    local_parts = lax.all_to_all(
        late_local[0].reshape(frag_rows, replicas, share_cols).transpose(1, 0, 2),
        "replica",
        0,
        0,
        tiled=True,
    )
    own_sum = jnp.sum(local_parts.astype(jnp.float32), axis=0)
    delta = frag_global - own_sum / replicas
    new_momentum = outer_momentum * frag_momentum + delta
    new_global = frag_global - outer_rate * (delta + outer_momentum * new_momentum)
    refreshed_parts = lax.all_to_all(
        jnp.broadcast_to(
            new_global.astype(jnp.bfloat16)[None], (replicas, frag_rows, share_cols)
        ),
        "replica",
        0,
        0,
        tiled=True,
    )
    refreshed_local = refreshed_parts.transpose(1, 0, 2).reshape(frag_rows, replicas * share_cols)
    value_groups = values_all.reshape(length_all, kv_heads, HD)
    context_heads = jnp.einsum(
        "ghts,sgd->tghd", probs_low, value_groups, preferred_element_type=jnp.float32
    ).astype(jnp.bfloat16)
    dprobs = jnp.einsum(
        "tghd,sgd->ghts", grad_heads, value_groups, preferred_element_type=jnp.float32
    )
    rowdot = jnp.sum(
        grad_heads.astype(jnp.float32) * context_heads.astype(jnp.float32), axis=-1
    ).transpose(1, 2, 0)[..., None]
    dscores = (probs * (dprobs - rowdot) * score_scale).astype(jnp.bfloat16)
    query_grad = (
        jnp.einsum("ghts,sgd->tghd", dscores, key_groups, preferred_element_type=jnp.float32)
        .astype(jnp.bfloat16)
        .reshape(tok_rows, queries.shape[1])
    )
    key_term = (
        jnp.einsum("ghts,tghd->sgd", dscores, query_heads, preferred_element_type=jnp.float32)
        .reshape(length_all, kv_width)
        .astype(jnp.bfloat16)
    )
    context = context_heads.reshape(tok_rows, queries.shape[1])
    key_term, token_source = lax.optimization_barrier((key_term, value_grad))
    key_parts = lax.all_to_all(
        key_term.reshape(fsdp_size, tok_rows, kv_width), "fsdp", 0, 0, tiled=True
    )
    key_grad = jnp.sum(key_parts.astype(jnp.float32), axis=0).astype(jnp.bfloat16)
    product = lax.dot_general(
        tokens, value_grad, (((0,), (0,)), ((), ())), preferred_element_type=jnp.float32
    )
    weight_term = (product * proj_scale).astype(jnp.bfloat16)
    weight_grad = lax.psum_scatter(
        weight_term, "fsdp", scatter_dimension=0, tiled=True
    ).astype(jnp.float32)
    token_sum = lax.dot_general(
        token_source,
        weight_all,
        (((1,), (1,)), ((), ())),
        preferred_element_type=jnp.float32,
    )
    token_grad = (token_sum * proj_scale).astype(jnp.bfloat16)
    return (
        context[None],
        query_grad[None],
        key_grad[None],
        weight_grad[None],
        token_grad[None],
        new_global,
        new_momentum,
        refreshed_local,
    )


def solution(mesh):
    return jax.shard_map(
        on_device,
        mesh=mesh,
        in_specs=(
            P("replica", "fsdp", None),
            P("replica", "fsdp", None),
            P("replica", "fsdp", None),
            P("fsdp", None),
            P("replica", "fsdp", None),
            P("fsdp", "replica"),
            P("fsdp", "replica"),
            P("replica", "fsdp", None),
        ),
        out_specs=(
            P("replica", "fsdp", None),
            P("replica", "fsdp", None),
            P("replica", "fsdp", None),
            P("replica", "fsdp", None),
            P("replica", "fsdp", None),
            P("fsdp", "replica"),
            P("fsdp", "replica"),
            P("fsdp", None),
        ),
        check_vma=False,
    )
```

```python
import jax
import jax.numpy as jnp
from jax import lax
from jax.sharding import PartitionSpec as P

HD = 128


outer_momentum = 0.9
outer_rate = 0.7
masked_score = -1e30


def on_device(
    tokens, queries, keys, value_weight, ctx_grad, frag_global, frag_momentum, frag_local
):
    tokens = tokens[0]
    queries = queries[0]
    keys = keys[0]
    ctx_grad = ctx_grad[0]
    tok_rows = tokens.shape[0]
    model_width = tokens.shape[1]
    proj_scale = model_width ** (-0.5)
    score_scale = HD ** (-0.5)
    kv_heads = keys.shape[1] // HD
    group = queries.shape[1] // (kv_heads * HD)
    key_rows = keys.shape[0]
    weight_rows = value_weight.shape[0]
    fsdp_size = lax.axis_size("fsdp")
    gathered = lax.all_gather(
        jnp.concatenate([keys, value_weight], axis=0), "fsdp", axis=0, tiled=False
    )
    keys_all = gathered[:, :key_rows].reshape(fsdp_size * key_rows, keys.shape[1])
    weight_all = gathered[:, key_rows:].reshape(fsdp_size * weight_rows, value_weight.shape[1])
    replicas = lax.axis_size("replica")
    share_cols = frag_global.shape[1]
    frag_rows = frag_global.shape[0]
    local_parts = lax.all_to_all(
        frag_local[0].reshape(frag_rows, replicas, share_cols).transpose(1, 0, 2),
        "replica",
        0,
        0,
        tiled=True,
    )
    own_sum = jnp.sum(local_parts.astype(jnp.float32), axis=0)
    delta = frag_global - own_sum / replicas
    new_momentum = outer_momentum * frag_momentum + delta
    new_global = frag_global - outer_rate * (delta + outer_momentum * new_momentum)
    refreshed_parts = lax.all_to_all(
        jnp.broadcast_to(
            new_global.astype(jnp.bfloat16)[None], (replicas, frag_rows, share_cols)
        ),
        "replica",
        0,
        0,
        tiled=True,
    )
    refreshed_local = refreshed_parts.transpose(1, 0, 2).reshape(frag_rows, replicas * share_cols)
    refreshed_local, keys_all = lax.optimization_barrier((refreshed_local, keys_all))
    value_sum = jnp.dot(tokens, weight_all, preferred_element_type=jnp.float32)
    values = (value_sum * proj_scale).astype(jnp.bfloat16)
    values_all = lax.all_gather(values, "fsdp", axis=0, tiled=True)
    length_all = keys_all.shape[0]
    query_pos = lax.axis_index("fsdp") * tok_rows + jnp.arange(tok_rows)
    causal = jnp.arange(length_all)[None, :] <= query_pos[:, None]
    query_heads = queries.reshape(tok_rows, kv_heads, group, HD)
    grad_heads = ctx_grad.reshape(tok_rows, kv_heads, group, HD)
    key_groups = keys_all.reshape(length_all, kv_heads, HD)
    scores = (
        jnp.einsum("tghd,sgd->ghts", query_heads, key_groups, preferred_element_type=jnp.float32)
        * score_scale
    )
    scores = jnp.where(causal[None, None], scores, masked_score)
    top = jnp.max(scores, axis=-1, keepdims=True)
    summed = jnp.sum(jnp.exp(scores - top), axis=-1, keepdims=True)
    log_total = top + jnp.log(summed)
    probs = jnp.exp(scores - log_total)
    probs_low = probs.astype(jnp.bfloat16)
    value_term = (
        jnp.einsum("ghts,tghd->sgd", probs_low, grad_heads, preferred_element_type=jnp.float32)
        .reshape(length_all, kv_heads * HD)
        .astype(jnp.bfloat16)
    )
    kv_width = value_term.shape[1]
    value_parts = lax.all_to_all(
        value_term.reshape(fsdp_size, tok_rows, kv_width), "fsdp", 0, 0, tiled=True
    )
    value_grad = jnp.sum(value_parts.astype(jnp.float32), axis=0).astype(jnp.bfloat16)
    value_groups = values_all.reshape(length_all, kv_heads, HD)
    context_heads = jnp.einsum(
        "ghts,sgd->tghd", probs_low, value_groups, preferred_element_type=jnp.float32
    ).astype(jnp.bfloat16)
    dprobs = jnp.einsum(
        "tghd,sgd->ghts", grad_heads, value_groups, preferred_element_type=jnp.float32
    )
    rowdot = jnp.sum(
        grad_heads.astype(jnp.float32) * context_heads.astype(jnp.float32), axis=-1
    ).transpose(1, 2, 0)[..., None]
    dscores = (probs * (dprobs - rowdot) * score_scale).astype(jnp.bfloat16)
    query_grad = (
        jnp.einsum("ghts,sgd->tghd", dscores, key_groups, preferred_element_type=jnp.float32)
        .astype(jnp.bfloat16)
        .reshape(tok_rows, queries.shape[1])
    )
    key_term = (
        jnp.einsum("ghts,tghd->sgd", dscores, query_heads, preferred_element_type=jnp.float32)
        .reshape(length_all, kv_width)
        .astype(jnp.bfloat16)
    )
    context = context_heads.reshape(tok_rows, queries.shape[1])
    key_term, token_source = lax.optimization_barrier((key_term, value_grad))
    key_parts = lax.all_to_all(
        key_term.reshape(fsdp_size, tok_rows, kv_width), "fsdp", 0, 0, tiled=True
    )
    key_grad = jnp.sum(key_parts.astype(jnp.float32), axis=0).astype(jnp.bfloat16)
    product = lax.dot_general(
        tokens, value_grad, (((0,), (0,)), ((), ())), preferred_element_type=jnp.float32
    )
    weight_term = (product * proj_scale).astype(jnp.bfloat16)
    split_cols = weight_term.shape[1] // 2
    weight_left = lax.psum_scatter(
        weight_term[:, :split_cols], "fsdp", scatter_dimension=0, tiled=True
    ).astype(jnp.float32)
    weight_parts = lax.all_to_all(
        weight_term[:, split_cols:].reshape(fsdp_size, weight_rows, split_cols),
        "fsdp",
        0,
        0,
        tiled=True,
    )
    weight_right = jnp.sum(weight_parts.astype(jnp.float32), axis=0)
    weight_grad = jnp.concatenate([weight_left, weight_right], axis=1)
    token_sum = lax.dot_general(
        token_source,
        weight_all,
        (((1,), (1,)), ((), ())),
        preferred_element_type=jnp.float32,
    )
    token_grad = (token_sum * proj_scale).astype(jnp.bfloat16)
    return (
        context[None],
        query_grad[None],
        key_grad[None],
        weight_grad[None],
        token_grad[None],
        new_global,
        new_momentum,
        refreshed_local,
    )


def solution(mesh):
    return jax.shard_map(
        on_device,
        mesh=mesh,
        in_specs=(
            P("replica", "fsdp", None),
            P("replica", "fsdp", None),
            P("replica", "fsdp", None),
            P("fsdp", None),
            P("replica", "fsdp", None),
            P("fsdp", "replica"),
            P("fsdp", "replica"),
            P("replica", "fsdp", None),
        ),
        out_specs=(
            P("replica", "fsdp", None),
            P("replica", "fsdp", None),
            P("replica", "fsdp", None),
            P("replica", "fsdp", None),
            P("replica", "fsdp", None),
            P("fsdp", "replica"),
            P("fsdp", "replica"),
            P("fsdp", None),
        ),
        check_vma=False,
    )
```

```python
import jax
import jax.numpy as jnp
from jax import lax
from jax.sharding import PartitionSpec as P

HD = 128


outer_momentum = 0.9
outer_rate = 0.7
masked_score = -1e30


def on_device(
    tokens, queries, keys, value_weight, ctx_grad, frag_global, frag_momentum, frag_local
):
    tokens = tokens[0]
    queries = queries[0]
    keys = keys[0]
    ctx_grad = ctx_grad[0]
    tok_rows = tokens.shape[0]
    model_width = tokens.shape[1]
    proj_scale = model_width ** (-0.5)
    score_scale = HD ** (-0.5)
    kv_heads = keys.shape[1] // HD
    group = queries.shape[1] // (kv_heads * HD)
    key_rows = keys.shape[0]
    weight_rows = value_weight.shape[0]
    fsdp_size = lax.axis_size("fsdp")
    gathered = lax.all_gather(
        jnp.concatenate([keys, value_weight], axis=0), "fsdp", axis=0, tiled=False
    )
    keys_all = gathered[:, :key_rows].reshape(fsdp_size * key_rows, keys.shape[1])
    weight_all = gathered[:, key_rows:].reshape(fsdp_size * weight_rows, value_weight.shape[1])
    replicas = lax.axis_size("replica")
    share_cols = frag_global.shape[1]
    frag_rows = frag_global.shape[0]
    local_parts = lax.all_to_all(
        frag_local[0].reshape(frag_rows, replicas, share_cols).transpose(1, 0, 2),
        "replica",
        0,
        0,
        tiled=True,
    )
    own_sum = jnp.sum(local_parts.astype(jnp.float32), axis=0)
    delta = frag_global - own_sum / replicas
    new_momentum = outer_momentum * frag_momentum + delta
    new_global = frag_global - outer_rate * (delta + outer_momentum * new_momentum)
    refreshed_parts = lax.all_to_all(
        jnp.broadcast_to(
            new_global.astype(jnp.bfloat16)[None], (replicas, frag_rows, share_cols)
        ),
        "replica",
        0,
        0,
        tiled=True,
    )
    refreshed_local = refreshed_parts.transpose(1, 0, 2).reshape(frag_rows, replicas * share_cols)
    refreshed_local, keys_all = lax.optimization_barrier((refreshed_local, keys_all))
    value_sum = jnp.dot(tokens, weight_all, preferred_element_type=jnp.float32)
    values = (value_sum * proj_scale).astype(jnp.bfloat16)
    values_all = lax.all_gather(values, "fsdp", axis=0, tiled=True)
    length_all = keys_all.shape[0]
    query_pos = lax.axis_index("fsdp") * tok_rows + jnp.arange(tok_rows)
    causal = jnp.arange(length_all)[None, :] <= query_pos[:, None]
    query_heads = queries.reshape(tok_rows, kv_heads, group, HD)
    grad_heads = ctx_grad.reshape(tok_rows, kv_heads, group, HD)
    key_groups = keys_all.reshape(length_all, kv_heads, HD)
    scores = (
        jnp.einsum("tghd,sgd->ghts", query_heads, key_groups, preferred_element_type=jnp.float32)
        * score_scale
    )
    scores = jnp.where(causal[None, None], scores, masked_score)
    top = jnp.max(scores, axis=-1, keepdims=True)
    summed = jnp.sum(jnp.exp(scores - top), axis=-1, keepdims=True)
    log_total = top + jnp.log(summed)
    probs = jnp.exp(scores - log_total)
    probs_low = probs.astype(jnp.bfloat16)
    value_term = (
        jnp.einsum("ghts,tghd->sgd", probs_low, grad_heads, preferred_element_type=jnp.float32)
        .reshape(length_all, kv_heads * HD)
        .astype(jnp.bfloat16)
    )
    kv_width = value_term.shape[1]
    value_parts = lax.all_to_all(
        value_term.reshape(fsdp_size, tok_rows, kv_width), "fsdp", 0, 0, tiled=True
    )
    value_grad = jnp.sum(value_parts.astype(jnp.float32), axis=0).astype(jnp.bfloat16)
    value_groups = values_all.reshape(length_all, kv_heads, HD)
    context_heads = jnp.einsum(
        "ghts,sgd->tghd", probs_low, value_groups, preferred_element_type=jnp.float32
    ).astype(jnp.bfloat16)
    dprobs = jnp.einsum(
        "tghd,sgd->ghts", grad_heads, value_groups, preferred_element_type=jnp.float32
    )
    rowdot = jnp.sum(
        grad_heads.astype(jnp.float32) * context_heads.astype(jnp.float32), axis=-1
    ).transpose(1, 2, 0)[..., None]
    dscores = (probs * (dprobs - rowdot) * score_scale).astype(jnp.bfloat16)
    query_grad = (
        jnp.einsum("ghts,sgd->tghd", dscores, key_groups, preferred_element_type=jnp.float32)
        .astype(jnp.bfloat16)
        .reshape(tok_rows, queries.shape[1])
    )
    key_term = (
        jnp.einsum("ghts,tghd->sgd", dscores, query_heads, preferred_element_type=jnp.float32)
        .reshape(length_all, kv_width)
        .astype(jnp.bfloat16)
    )
    context = context_heads.reshape(tok_rows, queries.shape[1])
    key_term, token_source = lax.optimization_barrier((key_term, value_grad))
    key_parts = lax.all_to_all(
        key_term.reshape(fsdp_size, tok_rows, kv_width), "fsdp", 0, 0, tiled=True
    )
    key_grad = jnp.sum(key_parts.astype(jnp.float32), axis=0).astype(jnp.bfloat16)
    product = lax.dot_general(
        tokens, value_grad, (((0,), (0,)), ((), ())), preferred_element_type=jnp.float32
    )
    weight_term = (product * proj_scale).astype(jnp.bfloat16)
    split_cols = weight_term.shape[1] // 4
    weight_left = lax.psum_scatter(
        weight_term[:, :split_cols], "fsdp", scatter_dimension=0, tiled=True
    ).astype(jnp.float32)
    weight_parts = lax.all_to_all(
        weight_term[:, split_cols:].reshape(fsdp_size, weight_rows, weight_term.shape[1] - split_cols),
        "fsdp",
        0,
        0,
        tiled=True,
    )
    weight_right = jnp.sum(weight_parts.astype(jnp.float32), axis=0)
    weight_grad = jnp.concatenate([weight_left, weight_right], axis=1)
    token_sum = lax.dot_general(
        token_source,
        weight_all,
        (((1,), (1,)), ((), ())),
        preferred_element_type=jnp.float32,
    )
    token_grad = (token_sum * proj_scale).astype(jnp.bfloat16)
    return (
        context[None],
        query_grad[None],
        key_grad[None],
        weight_grad[None],
        token_grad[None],
        new_global,
        new_momentum,
        refreshed_local,
    )


def solution(mesh):
    return jax.shard_map(
        on_device,
        mesh=mesh,
        in_specs=(
            P("replica", "fsdp", None),
            P("replica", "fsdp", None),
            P("replica", "fsdp", None),
            P("fsdp", None),
            P("replica", "fsdp", None),
            P("fsdp", "replica"),
            P("fsdp", "replica"),
            P("replica", "fsdp", None),
        ),
        out_specs=(
            P("replica", "fsdp", None),
            P("replica", "fsdp", None),
            P("replica", "fsdp", None),
            P("replica", "fsdp", None),
            P("replica", "fsdp", None),
            P("fsdp", "replica"),
            P("fsdp", "replica"),
            P("fsdp", None),
        ),
        check_vma=False,
    )
```

```python
import jax
import jax.numpy as jnp
from jax import lax
from jax.sharding import PartitionSpec as P

HD = 128


outer_momentum = 0.9
outer_rate = 0.7
masked_score = -1e30


def on_device(
    tokens, queries, keys, value_weight, ctx_grad, frag_global, frag_momentum, frag_local
):
    tokens = tokens[0]
    queries = queries[0]
    keys = keys[0]
    ctx_grad = ctx_grad[0]
    tok_rows = tokens.shape[0]
    model_width = tokens.shape[1]
    proj_scale = model_width ** (-0.5)
    score_scale = HD ** (-0.5)
    kv_heads = keys.shape[1] // HD
    group = queries.shape[1] // (kv_heads * HD)
    key_rows = keys.shape[0]
    weight_rows = value_weight.shape[0]
    fsdp_size = lax.axis_size("fsdp")
    keys_all = lax.all_to_all(
        jnp.broadcast_to(keys[None], (fsdp_size, key_rows, keys.shape[1])),
        "fsdp",
        0,
        0,
        tiled=True,
    ).reshape(fsdp_size * key_rows, keys.shape[1])
    weight_all = lax.all_gather(value_weight, "fsdp", axis=0, tiled=True)
    replicas = lax.axis_size("replica")
    share_cols = frag_global.shape[1]
    frag_rows = frag_global.shape[0]
    local_parts = lax.all_to_all(
        frag_local[0].reshape(frag_rows, replicas, share_cols).transpose(1, 0, 2),
        "replica",
        0,
        0,
        tiled=True,
    )
    own_sum = jnp.sum(local_parts.astype(jnp.float32), axis=0)
    delta = frag_global - own_sum / replicas
    new_momentum = outer_momentum * frag_momentum + delta
    new_global = frag_global - outer_rate * (delta + outer_momentum * new_momentum)
    refreshed_parts = lax.all_to_all(
        jnp.broadcast_to(
            new_global.astype(jnp.bfloat16)[None], (replicas, frag_rows, share_cols)
        ),
        "replica",
        0,
        0,
        tiled=True,
    )
    refreshed_local = refreshed_parts.transpose(1, 0, 2).reshape(frag_rows, replicas * share_cols)
    refreshed_local, keys_all = lax.optimization_barrier((refreshed_local, keys_all))
    value_sum = jnp.dot(tokens, weight_all, preferred_element_type=jnp.float32)
    values = (value_sum * proj_scale).astype(jnp.bfloat16)
    values_all = lax.all_gather(values, "fsdp", axis=0, tiled=True)
    length_all = keys_all.shape[0]
    query_pos = lax.axis_index("fsdp") * tok_rows + jnp.arange(tok_rows)
    causal = jnp.arange(length_all)[None, :] <= query_pos[:, None]
    query_heads = queries.reshape(tok_rows, kv_heads, group, HD)
    grad_heads = ctx_grad.reshape(tok_rows, kv_heads, group, HD)
    key_groups = keys_all.reshape(length_all, kv_heads, HD)
    scores = (
        jnp.einsum("tghd,sgd->ghts", query_heads, key_groups, preferred_element_type=jnp.float32)
        * score_scale
    )
    scores = jnp.where(causal[None, None], scores, masked_score)
    top = jnp.max(scores, axis=-1, keepdims=True)
    summed = jnp.sum(jnp.exp(scores - top), axis=-1, keepdims=True)
    log_total = top + jnp.log(summed)
    probs = jnp.exp(scores - log_total)
    probs_low = probs.astype(jnp.bfloat16)
    value_term = (
        jnp.einsum("ghts,tghd->sgd", probs_low, grad_heads, preferred_element_type=jnp.float32)
        .reshape(length_all, kv_heads * HD)
        .astype(jnp.bfloat16)
    )
    kv_width = value_term.shape[1]
    value_parts = lax.all_to_all(
        value_term.reshape(fsdp_size, tok_rows, kv_width), "fsdp", 0, 0, tiled=True
    )
    value_grad = jnp.sum(value_parts.astype(jnp.float32), axis=0).astype(jnp.bfloat16)
    value_groups = values_all.reshape(length_all, kv_heads, HD)
    context_heads = jnp.einsum(
        "ghts,sgd->tghd", probs_low, value_groups, preferred_element_type=jnp.float32
    ).astype(jnp.bfloat16)
    dprobs = jnp.einsum(
        "tghd,sgd->ghts", grad_heads, value_groups, preferred_element_type=jnp.float32
    )
    rowdot = jnp.sum(
        grad_heads.astype(jnp.float32) * context_heads.astype(jnp.float32), axis=-1
    ).transpose(1, 2, 0)[..., None]
    dscores = (probs * (dprobs - rowdot) * score_scale).astype(jnp.bfloat16)
    query_grad = (
        jnp.einsum("ghts,sgd->tghd", dscores, key_groups, preferred_element_type=jnp.float32)
        .astype(jnp.bfloat16)
        .reshape(tok_rows, queries.shape[1])
    )
    key_term = (
        jnp.einsum("ghts,tghd->sgd", dscores, query_heads, preferred_element_type=jnp.float32)
        .reshape(length_all, kv_width)
        .astype(jnp.bfloat16)
    )
    context = context_heads.reshape(tok_rows, queries.shape[1])
    key_term, token_source = lax.optimization_barrier((key_term, value_grad))
    key_parts = lax.all_to_all(
        key_term.reshape(fsdp_size, tok_rows, kv_width), "fsdp", 0, 0, tiled=True
    )
    key_grad = jnp.sum(key_parts.astype(jnp.float32), axis=0).astype(jnp.bfloat16)
    product = lax.dot_general(
        tokens, value_grad, (((0,), (0,)), ((), ())), preferred_element_type=jnp.float32
    )
    weight_term = (product * proj_scale).astype(jnp.bfloat16)
    split_cols = weight_term.shape[1] // 2
    weight_left = lax.psum_scatter(
        weight_term[:, :split_cols], "fsdp", scatter_dimension=0, tiled=True
    ).astype(jnp.float32)
    weight_parts = lax.all_to_all(
        weight_term[:, split_cols:].reshape(fsdp_size, weight_rows, split_cols),
        "fsdp",
        0,
        0,
        tiled=True,
    )
    weight_right = jnp.sum(weight_parts.astype(jnp.float32), axis=0)
    weight_grad = jnp.concatenate([weight_left, weight_right], axis=1)
    token_sum = lax.dot_general(
        token_source,
        weight_all,
        (((1,), (1,)), ((), ())),
        preferred_element_type=jnp.float32,
    )
    token_grad = (token_sum * proj_scale).astype(jnp.bfloat16)
    return (
        context[None],
        query_grad[None],
        key_grad[None],
        weight_grad[None],
        token_grad[None],
        new_global,
        new_momentum,
        refreshed_local,
    )


def solution(mesh):
    return jax.shard_map(
        on_device,
        mesh=mesh,
        in_specs=(
            P("replica", "fsdp", None),
            P("replica", "fsdp", None),
            P("replica", "fsdp", None),
            P("fsdp", None),
            P("replica", "fsdp", None),
            P("fsdp", "replica"),
            P("fsdp", "replica"),
            P("replica", "fsdp", None),
        ),
        out_specs=(
            P("replica", "fsdp", None),
            P("replica", "fsdp", None),
            P("replica", "fsdp", None),
            P("replica", "fsdp", None),
            P("replica", "fsdp", None),
            P("fsdp", "replica"),
            P("fsdp", "replica"),
            P("fsdp", None),
        ),
        check_vma=False,
    )
```

```python
import jax
import jax.numpy as jnp
from jax import lax
from jax.sharding import PartitionSpec as P

HD = 128


outer_momentum = 0.9
outer_rate = 0.7
masked_score = -1e30


def on_device(
    tokens, queries, keys, value_weight, ctx_grad, frag_global, frag_momentum, frag_local
):
    tokens = tokens[0]
    queries = queries[0]
    keys = keys[0]
    ctx_grad = ctx_grad[0]
    tok_rows = tokens.shape[0]
    model_width = tokens.shape[1]
    proj_scale = model_width ** (-0.5)
    score_scale = HD ** (-0.5)
    kv_heads = keys.shape[1] // HD
    group = queries.shape[1] // (kv_heads * HD)
    key_rows = keys.shape[0]
    weight_rows = value_weight.shape[0]
    fsdp_size = lax.axis_size("fsdp")
    gathered = lax.all_gather(
        jnp.concatenate([keys, value_weight], axis=0), "fsdp", axis=0, tiled=False
    )
    keys_all = gathered[:, :key_rows].reshape(fsdp_size * key_rows, keys.shape[1])
    weight_all = gathered[:, key_rows:].reshape(fsdp_size * weight_rows, value_weight.shape[1])
    replicas = lax.axis_size("replica")
    share_cols = frag_global.shape[1]
    frag_rows = frag_global.shape[0]
    local_parts = lax.all_to_all(
        frag_local[0].reshape(frag_rows, replicas, share_cols).transpose(1, 0, 2),
        "replica",
        0,
        0,
        tiled=True,
    )
    own_sum = jnp.sum(local_parts.astype(jnp.float32), axis=0)
    delta = frag_global - own_sum / replicas
    new_momentum = outer_momentum * frag_momentum + delta
    new_global = frag_global - outer_rate * (delta + outer_momentum * new_momentum)
    refreshed_parts = lax.all_to_all(
        jnp.broadcast_to(
            new_global.astype(jnp.bfloat16)[None], (replicas, frag_rows, share_cols)
        ),
        "replica",
        0,
        0,
        tiled=True,
    )
    refreshed_local = refreshed_parts.transpose(1, 0, 2).reshape(frag_rows, replicas * share_cols)
    refreshed_local, keys_all = lax.optimization_barrier((refreshed_local, keys_all))
    value_sum = jnp.dot(tokens, weight_all, preferred_element_type=jnp.float32)
    values = (value_sum * proj_scale).astype(jnp.bfloat16)
    values_all = lax.all_gather(values, "fsdp", axis=0, tiled=True)
    length_all = keys_all.shape[0]
    query_pos = lax.axis_index("fsdp") * tok_rows + jnp.arange(tok_rows)
    causal = jnp.arange(length_all)[None, :] <= query_pos[:, None]
    query_heads = queries.reshape(tok_rows, kv_heads, group, HD)
    grad_heads = ctx_grad.reshape(tok_rows, kv_heads, group, HD)
    key_groups = keys_all.reshape(length_all, kv_heads, HD)
    scores = (
        jnp.einsum("tghd,sgd->ghts", query_heads, key_groups, preferred_element_type=jnp.float32)
        * score_scale
    )
    scores = jnp.where(causal[None, None], scores, masked_score)
    top = jnp.max(scores, axis=-1, keepdims=True)
    summed = jnp.sum(jnp.exp(scores - top), axis=-1, keepdims=True)
    log_total = top + jnp.log(summed)
    probs = jnp.exp(scores - log_total)
    probs_low = probs.astype(jnp.bfloat16)
    value_term = (
        jnp.einsum("ghts,tghd->sgd", probs_low, grad_heads, preferred_element_type=jnp.float32)
        .reshape(length_all, kv_heads * HD)
        .astype(jnp.bfloat16)
    )
    kv_width = value_term.shape[1]
    value_parts = lax.all_to_all(
        value_term.reshape(fsdp_size, tok_rows, kv_width), "fsdp", 0, 0, tiled=True
    )
    value_grad = jnp.sum(value_parts.astype(jnp.float32), axis=0).astype(jnp.bfloat16)
    value_groups = values_all.reshape(length_all, kv_heads, HD)
    context_heads = jnp.einsum(
        "ghts,sgd->tghd", probs_low, value_groups, preferred_element_type=jnp.float32
    ).astype(jnp.bfloat16)
    dprobs = jnp.einsum(
        "tghd,sgd->ghts", grad_heads, value_groups, preferred_element_type=jnp.float32
    )
    rowdot = jnp.sum(
        grad_heads.astype(jnp.float32) * context_heads.astype(jnp.float32), axis=-1
    ).transpose(1, 2, 0)[..., None]
    dscores = (probs * (dprobs - rowdot) * score_scale).astype(jnp.bfloat16)
    query_grad = (
        jnp.einsum("ghts,sgd->tghd", dscores, key_groups, preferred_element_type=jnp.float32)
        .astype(jnp.bfloat16)
        .reshape(tok_rows, queries.shape[1])
    )
    key_term = (
        jnp.einsum("ghts,tghd->sgd", dscores, query_heads, preferred_element_type=jnp.float32)
        .reshape(length_all, kv_width)
        .astype(jnp.bfloat16)
    )
    context = context_heads.reshape(tok_rows, queries.shape[1])
    key_term, token_source = lax.optimization_barrier((key_term, value_grad))
    key_parts = lax.all_to_all(
        key_term.reshape(fsdp_size, tok_rows, kv_width), "fsdp", 0, 0, tiled=True
    )
    key_grad = jnp.sum(key_parts.astype(jnp.float32), axis=0).astype(jnp.bfloat16)
    product = lax.dot_general(
        tokens, value_grad, (((0,), (0,)), ((), ())), preferred_element_type=jnp.float32
    )
    weight_term = (product * proj_scale).astype(jnp.bfloat16)
    split_cols = weight_term.shape[1] * 3 // 4
    weight_left = lax.psum_scatter(
        weight_term[:, :split_cols], "fsdp", scatter_dimension=0, tiled=True
    ).astype(jnp.float32)
    weight_parts = lax.all_to_all(
        weight_term[:, split_cols:].reshape(fsdp_size, weight_rows, weight_term.shape[1] - split_cols),
        "fsdp",
        0,
        0,
        tiled=True,
    )
    weight_right = jnp.sum(weight_parts.astype(jnp.float32), axis=0)
    weight_grad = jnp.concatenate([weight_left, weight_right], axis=1)
    token_sum = lax.dot_general(
        token_source,
        weight_all,
        (((1,), (1,)), ((), ())),
        preferred_element_type=jnp.float32,
    )
    token_grad = (token_sum * proj_scale).astype(jnp.bfloat16)
    return (
        context[None],
        query_grad[None],
        key_grad[None],
        weight_grad[None],
        token_grad[None],
        new_global,
        new_momentum,
        refreshed_local,
    )


def solution(mesh):
    return jax.shard_map(
        on_device,
        mesh=mesh,
        in_specs=(
            P("replica", "fsdp", None),
            P("replica", "fsdp", None),
            P("replica", "fsdp", None),
            P("fsdp", None),
            P("replica", "fsdp", None),
            P("fsdp", "replica"),
            P("fsdp", "replica"),
            P("replica", "fsdp", None),
        ),
        out_specs=(
            P("replica", "fsdp", None),
            P("replica", "fsdp", None),
            P("replica", "fsdp", None),
            P("replica", "fsdp", None),
            P("replica", "fsdp", None),
            P("fsdp", "replica"),
            P("fsdp", "replica"),
            P("fsdp", None),
        ),
        check_vma=False,
    )
```
